32 devices in a mesh: elem: 8 (over z, x), cuts: 4 (over y, core).
Axes of the slice: x: 2, y: 2, z: 4, core: 2. Of those that a mesh axis runs over, the one named last changes fastest.
Arguments:
- basis: bfloat16 [8, 32768, 160], P('elem', 'cuts'), may hold values from -6 to 6
- quad_weight: float32 [8, 32768], P('elem', 'cuts'), may hold values from 0.5 to 2
- projectors: bfloat16 [8, 3, 20, 16, 32768], P('elem', None, None, None, 'cuts'), may hold values from -0.03125 to 0.03125
- species: int32 [8, 20], P('elem'), may hold values from 0 to 3
- counts: int32 [8, 20], P('elem'), may hold values from 1 to 16
- gamma_table: float32 [4, 16], replicated, may hold values from -0.4375 to 0.4375
Outputs:
- blocks: float32 [8, 3, 160, 160], P(None, None, 'elem', 'cuts')
The draws below stay inside these ranges and needn't reach their ends.
Inputs may be any that keep to these rules, and one draw needn't show every extreme that they name: `counts`: each atom has at least one projector and at most 16.
All inputs are finite; a program needn't handle non-finite values.
Results may differ from the reference program's by a relative error of at most 0.004.
Values sent between devices are 32-bit elements; how exact they have to be, the bound alone decides.
No kernel may reach another device: no remote copies, remote signals or barrier semaphores. Data moves between devices by JAX's collectives and lax.ppermute only.
A program may use at most 64 MiB of HBM per device.

```python
import math
import jax
import jax.numpy as jnp
from jax import lax

BASIS = 160
PROJ = 16
SPECIES = 4
HOME = 20
ELEMENTS = 8
POINTS = 32768


def plant(values, rng, low, high):
    dims = values.shape
    spot = [jax.random.randint(jax.random.fold_in(rng, axis), (), 0, dims[axis]) for axis in range(len(dims))]
    values = values.at[tuple(spot)].set(low)
    longest = dims.index(max(dims))
    spot[longest] = (spot[longest] + 1) % dims[longest]
    return values.at[tuple(spot)].set(high)


def block_levels(stream_key, extent, pieces, low, high):
    def one(position, shards_of):
        steps = jax.random.uniform(jax.random.fold_in(jax.random.fold_in(stream_key, 6), position), (shards_of,), jnp.float32, low / len(pieces), high / len(pieces))
        return jnp.repeat(jnp.exp(steps), extent[position] // shards_of).reshape((-1,) + (1,) * (len(extent) - position - 1))

    factor_of = one(*pieces[0])
    for cut in pieces[1:]:
        factor_of = factor_of * one(*cut)
    return factor_of


def noise(key, extent, spread, reach, cuts=(), kind=jnp.bfloat16):
    values = jax.random.normal(key, extent, jnp.float32) * spread
    if len(cuts) > 0:
        values = block_levels(key, extent, cuts, -0.22, 0.18) * values
    return jnp.clip(values, min=-reach, max=reach).astype(kind)


def setup_inputs(seed: int = 0) -> dict:
    streams_of = jax.random.split(jax.random.key(seed), 7)
    basis = noise(streams_of[0], (ELEMENTS, POINTS, BASIS), 1.0, 6.0, ((0, 8), (1, 4)))
    quad_weight = jnp.clip(jnp.exp(math.log(2.0) - 1.3862944 * jax.random.uniform(streams_of[1], (ELEMENTS, POINTS), jnp.float32) ** block_levels(streams_of[1], (ELEMENTS, POINTS), ((0, 8), (1, 4)), -0.2, 0.2)), 0.5, 2.0)
    projectors = noise(streams_of[2], (ELEMENTS, 3, HOME, PROJ, POINTS), POINTS ** -0.5, 0.03125, ((0, 8), (4, 4)))
    species = plant(jax.random.randint(streams_of[3], (ELEMENTS, HOME), 0, SPECIES), jax.random.fold_in(streams_of[3], 1), 0, SPECIES - 1).astype(jnp.int32)
    counts = plant(jax.random.randint(streams_of[4], (ELEMENTS, HOME), 1, PROJ + 1), jax.random.fold_in(streams_of[4], 1), 1, PROJ).astype(jnp.int32)
    gamma_table = noise(streams_of[5], (SPECIES, PROJ), 0.03, 0.4375, (), jnp.float32)
    return dict(basis=basis, quad_weight=quad_weight, projectors=projectors, species=species, counts=counts, gamma_table=gamma_table)


def pair_block(left, weights, right):
    scaled_left = left * weights[:, :, None]
    return jnp.einsum('eib,eic->ebc', scaled_left, right, precision=lax.Precision.HIGHEST)


def reference(basis, quad_weight, projectors, species, counts, gamma_table):
    scaled = (basis.astype(jnp.float32) * quad_weight[:, :, None]).astype(jnp.bfloat16)
    span = HOME * PROJ

    def element_coeffs(items):
        proj_elem, basis_elem = items
        flat = proj_elem.reshape(3 * span, POINTS)
        return jnp.dot(flat, basis_elem, preferred_element_type=jnp.float32).reshape(3, span, BASIS)

    coeffs = lax.map(element_coeffs, (projectors, scaled))
    onehot = (species[:, :, None] == jnp.arange(SPECIES, dtype=jnp.int32)[None, None, :]).astype(jnp.float32)
    table = jnp.einsum('eas,sl->eal', onehot, gamma_table, precision=lax.Precision.HIGHEST)
    active = (jnp.arange(PROJ, dtype=jnp.int32)[None, None, :] < counts[:, :, None]).astype(jnp.float32)
    energy = (table * active).reshape(ELEMENTS, span)
    energy_left = jnp.roll(energy, 1, axis=0)
    energy_right = jnp.roll(energy, -1, axis=0)
    from_left = jnp.roll(coeffs, 1, axis=0)
    from_right = jnp.roll(coeffs, -1, axis=0)
    group0, group1, group2 = coeffs[:, 0], coeffs[:, 1], coeffs[:, 2]
    block_left = pair_block(group0, energy_left, from_left[:, 1]) + pair_block(group1, energy, from_left[:, 2])
    block_diag = (pair_block(group0, energy_left, group0) + pair_block(group1, energy, group1)
                  + pair_block(group2, energy_right, group2))
    block_right = pair_block(group1, energy, from_right[:, 0]) + pair_block(group2, energy_right, from_right[:, 1])
    return jnp.stack([block_left, block_diag, block_right], axis=1)
```

```python
import jax
import jax.numpy as jnp
from jax import lax
from jax.sharding import PartitionSpec as P


def passed_along(block, axis, distance):
    devices = range(lax.axis_size(axis))
    route = [((i - distance) % len(devices), i) for i in devices]
    return lax.ppermute(block, axis, route)


def swapped(block, axis, bit):
    devices = range(lax.axis_size(axis))
    return lax.ppermute(block, axis, [(i, i ^ bit) for i in devices])


def reduce_scatter_columns(partial_value, axis, quarter):
    rows = partial_value.shape[0]
    size = lax.axis_size(axis)
    me = lax.axis_index(axis)
    held = partial_value.reshape(rows, size, quarter)
    bit = 1
    while bit < size:
        pairs = held.reshape(rows, held.shape[1] // 2, 2, quarter)
        mine = (me & bit) != 0
        keep = jnp.where(mine, pairs[:, :, 1], pairs[:, :, 0])
        send = jnp.where(mine, pairs[:, :, 0], pairs[:, :, 1])
        held = keep + swapped(send, axis, bit)
        bit *= 2
    return held.reshape(rows, quarter)


def all_gather_columns(share, axis):
    rows, quarter = share.shape
    size = lax.axis_size(axis)
    me = lax.axis_index(axis)
    held = share.reshape(rows, 1, quarter)
    bit = size // 2
    while bit >= 1:
        other = swapped(held, axis, bit)
        mine = (me & bit) != 0
        low = jnp.where(mine, other, held)
        high = jnp.where(mine, held, other)
        held = jnp.stack([low, high], axis=2).reshape(rows, held.shape[1] * 2, quarter)
        bit //= 2
    return held.reshape(rows, size * quarter)


def pair_block(left, right):
    return jnp.einsum("ib,ic->bc", left, right, precision=lax.Precision.HIGHEST)


def local(basis, quad_weight, projectors, species, counts, gamma_table):
    width = basis.shape[2]
    groups, atoms, slots, points = projectors.shape[1:]
    span = atoms * slots
    quarter = width // lax.axis_size("cuts")
    scaled = (basis[0].astype(jnp.float32) * quad_weight[0][:, None]).astype(jnp.bfloat16)
    partial_value = jnp.dot(
        projectors[0].reshape(groups * span, points), scaled, preferred_element_type=jnp.float32
    )
    onehot = (
        species[0][:, None] == jnp.arange(gamma_table.shape[0], dtype=jnp.int32)[None, :]
    ).astype(jnp.float32)
    table = jnp.dot(onehot, gamma_table, precision=lax.Precision.HIGHEST)
    active = (jnp.arange(slots, dtype=jnp.int32)[None, :] < counts[0][:, None]).astype(jnp.float32)
    energy = (table * active).reshape(span)

    share = reduce_scatter_columns(partial_value, "cuts", quarter)
    energy_rows = -(-span // quarter)
    packed_energy = jnp.pad(energy, (0, energy_rows * quarter - span)).reshape(energy_rows, quarter)
    to_right = jnp.concatenate([share[span:], packed_energy], axis=0)
    to_left = jnp.concatenate([share[: 2 * span], packed_energy], axis=0)
    from_left = passed_along(to_right, "elem", 1)
    from_right = passed_along(to_left, "elem", -1)
    full = all_gather_columns(share, "cuts")

    left_energy = from_left[2 * span :].reshape(-1)[:span]
    right_energy = from_right[2 * span :].reshape(-1)[:span]
    weight_left = jnp.concatenate([left_energy, energy])
    weight_diag = jnp.concatenate([left_energy, energy, right_energy])
    weight_right = jnp.concatenate([energy, right_energy])
    block_left = pair_block(full[: 2 * span], weight_left[:, None] * from_left[: 2 * span])
    block_diag = pair_block(full, weight_diag[:, None] * share)
    block_right = pair_block(full[span:], weight_right[:, None] * from_right[: 2 * span])
    stacked = jnp.stack([block_left, block_diag, block_right], axis=0)[None]
    return lax.all_to_all(stacked, "elem", split_axis=2, concat_axis=0, tiled=True)


def solution(mesh):
    in_specs = (
        P("elem", "cuts", None),
        P("elem", "cuts"),
        P("elem", None, None, None, "cuts"),
        P("elem", None),
        P("elem", None),
        P(),
    )
    out_specs = P(None, None, "elem", "cuts")
    return jax.shard_map(local, mesh=mesh, in_specs=in_specs, out_specs=out_specs, check_vma=False)
```

```python
import jax
import jax.numpy as jnp
from jax import lax
from jax.sharding import PartitionSpec as P


def passed_along(block, axis, distance):
    devices = range(lax.axis_size(axis))
    route = [((i - distance) % len(devices), i) for i in devices]
    return lax.ppermute(block, axis, route)


def swapped(block, axis, bit):
    devices = range(lax.axis_size(axis))
    return lax.ppermute(block, axis, [(i, i ^ bit) for i in devices])


def summed_columns(partial_value, axis, quarter):
    rows = partial_value.shape[0]
    size = lax.axis_size(axis)
    me = lax.axis_index(axis)
    pairs = partial_value.reshape(rows, size // 2, 2, quarter)
    odd = (me & 1) != 0
    keep = jnp.where(odd, pairs[:, :, 1], pairs[:, :, 0])
    send = jnp.where(odd, pairs[:, :, 0], pairs[:, :, 1])
    half = keep + swapped(send, axis, 1)
    bit = 2
    while bit < size:
        half = half + swapped(half, axis, bit)
        bit *= 2
    share = lax.dynamic_index_in_dim(half, me // 2, 1, keepdims=False)
    return half, share


def gathered_columns(half, axis):
    rows, count, quarter = half.shape
    odd = (lax.axis_index(axis) & 1) != 0
    other = swapped(half, axis, 1)
    low = jnp.where(odd, other, half)
    high = jnp.where(odd, half, other)
    return jnp.stack([low, high], axis=2).reshape(rows, count * 2 * quarter)


def pair_block(left, right):
    return jnp.einsum("ib,ic->bc", left, right, precision=lax.Precision.HIGHEST)


def local(basis, quad_weight, projectors, species, counts, gamma_table):
    width = basis.shape[2]
    groups, atoms, slots, points = projectors.shape[1:]
    span = atoms * slots
    quarter = width // lax.axis_size("cuts")
    scaled = (basis[0].astype(jnp.float32) * quad_weight[0][:, None]).astype(jnp.bfloat16)
    partial_value = jnp.dot(
        projectors[0].reshape(groups * span, points), scaled, preferred_element_type=jnp.float32
    )
    onehot = (
        species[0][:, None] == jnp.arange(gamma_table.shape[0], dtype=jnp.int32)[None, :]
    ).astype(jnp.float32)
    table = jnp.dot(onehot, gamma_table, precision=lax.Precision.HIGHEST)
    active = (jnp.arange(slots, dtype=jnp.int32)[None, :] < counts[0][:, None]).astype(jnp.float32)
    energy = (table * active).reshape(span)

    half, share = summed_columns(partial_value, "cuts", quarter)
    energy_rows = -(-span // quarter)
    packed_energy = jnp.pad(energy, (0, energy_rows * quarter - span)).reshape(energy_rows, quarter)
    to_right = jnp.concatenate([share[span:], packed_energy], axis=0)
    to_left = jnp.concatenate([share[: 2 * span], packed_energy], axis=0)
    from_left = passed_along(to_right, "elem", 1)
    from_right = passed_along(to_left, "elem", -1)
    full = gathered_columns(half, "cuts")

    left_energy = from_left[2 * span :].reshape(-1)[:span]
    right_energy = from_right[2 * span :].reshape(-1)[:span]
    weight_left = jnp.concatenate([left_energy, energy])
    weight_diag = jnp.concatenate([left_energy, energy, right_energy])
    weight_right = jnp.concatenate([energy, right_energy])
    block_left = pair_block(full[: 2 * span], weight_left[:, None] * from_left[: 2 * span])
    block_diag = pair_block(full, weight_diag[:, None] * share)
    block_right = pair_block(full[span:], weight_right[:, None] * from_right[: 2 * span])
    owners = lax.axis_size("elem")
    stacked = jnp.stack([block_left, block_diag, block_right], axis=0)
    pieces = stacked.reshape(3, owners, width // owners, quarter).transpose(1, 0, 2, 3)
    return lax.all_to_all(pieces, "elem", split_axis=0, concat_axis=0, tiled=True)


def solution(mesh):
    in_specs = (
        P("elem", "cuts", None),
        P("elem", "cuts"),
        P("elem", None, None, None, "cuts"),
        P("elem", None),
        P("elem", None),
        P(),
    )
    out_specs = P(None, None, "elem", "cuts")
    return jax.shard_map(local, mesh=mesh, in_specs=in_specs, out_specs=out_specs, check_vma=False)
```

```python
import jax
import jax.numpy as jnp
from jax import lax
from jax.experimental import pallas as pl
from jax.experimental.pallas import tpu as pltpu
from jax.sharding import PartitionSpec as P


def passed_along(block, axis, distance):
    devices = range(lax.axis_size(axis))
    route = [((i - distance) % len(devices), i) for i in devices]
    return lax.ppermute(block, axis, route)


def swapped(block, axis, bit):
    devices = range(lax.axis_size(axis))
    return lax.ppermute(block, axis, [(i, i ^ bit) for i in devices])


def summed_columns(partial_value, axis, quarter):
    rows = partial_value.shape[0]
    size = lax.axis_size(axis)
    me = lax.axis_index(axis)
    pairs = partial_value.reshape(rows, size // 2, 2, quarter)
    odd = (me & 1) != 0
    keep = jnp.where(odd, pairs[:, :, 1], pairs[:, :, 0])
    send = jnp.where(odd, pairs[:, :, 0], pairs[:, :, 1])
    half = keep + swapped(send, axis, 1)
    bit = 2
    while bit < size:
        half = half + swapped(half, axis, bit)
        bit *= 2
    share = lax.dynamic_index_in_dim(half, me // 2, 1, keepdims=False)
    return half, share


def gathered_columns(half, axis):
    rows, count, quarter = half.shape
    odd = (lax.axis_index(axis) & 1) != 0
    other = swapped(half, axis, 1)
    low = jnp.where(odd, other, half)
    high = jnp.where(odd, half, other)
    return jnp.stack([low, high], axis=2).reshape(rows, count * 2 * quarter)


def coefficient_kernel(weight_ref, basis_ref, projector_ref, out_ref):
    step = pl.program_id(0)
    depth = weight_ref.shape[1]
    column = jnp.transpose(jnp.broadcast_to(weight_ref[...], (8, depth)))[:, :1]
    scaled = (basis_ref[...].astype(jnp.float32) * column).astype(jnp.bfloat16)
    product = jnp.dot(projector_ref[...], scaled, preferred_element_type=jnp.float32)

    @pl.when(step == 0)
    def _():
        out_ref[...] = product

    @pl.when(step > 0)
    def _():
        out_ref[...] += product


def partial_coefficients(flat_projectors, basis, weight):
    rows, points = flat_projectors.shape
    width = basis.shape[1]
    depth = min(points, 1024)
    return pl.pallas_call(
        coefficient_kernel,
        out_shape=jax.ShapeDtypeStruct((rows, width), jnp.float32),
        grid=(points // depth,),
        in_specs=[
            pl.BlockSpec((1, depth), lambda k: (0, k)),
            pl.BlockSpec((depth, width), lambda k: (k, 0)),
            pl.BlockSpec((rows, depth), lambda k: (0, k)),
        ],
        out_specs=pl.BlockSpec((rows, width), lambda k: (0, 0)),
        compiler_params=pltpu.CompilerParams(dimension_semantics=("arbitrary",)),
        cost_estimate=pl.CostEstimate(
            flops=2 * rows * points * width,
            bytes_accessed=2 * rows * points + 2 * points * width + 4 * points + 4 * rows * width,
            transcendentals=0,
        ),
    )(weight.reshape(1, points), basis, flat_projectors)


def pair_block(left, right):
    return jnp.einsum("ib,ic->bc", left, right, precision=lax.Precision.HIGHEST)


def local(basis, quad_weight, projectors, species, counts, gamma_table):
    width = basis.shape[2]
    groups, atoms, slots, points = projectors.shape[1:]
    span = atoms * slots
    quarter = width // lax.axis_size("cuts")
    partial_value = partial_coefficients(
        projectors[0].reshape(groups * span, points), basis[0], quad_weight[0]
    )
    onehot = (
        species[0][:, None] == jnp.arange(gamma_table.shape[0], dtype=jnp.int32)[None, :]
    ).astype(jnp.float32)
    table = jnp.dot(onehot, gamma_table, precision=lax.Precision.HIGHEST)
    active = (jnp.arange(slots, dtype=jnp.int32)[None, :] < counts[0][:, None]).astype(jnp.float32)
    energy = (table * active).reshape(span)

    half, share = summed_columns(partial_value, "cuts", quarter)
    energy_rows = -(-span // quarter)
    packed_energy = jnp.pad(energy, (0, energy_rows * quarter - span)).reshape(energy_rows, quarter)
    to_right = jnp.concatenate([share[span:], packed_energy], axis=0)
    to_left = jnp.concatenate([share[: 2 * span], packed_energy], axis=0)
    from_left = passed_along(to_right, "elem", 1)
    from_right = passed_along(to_left, "elem", -1)
    full = gathered_columns(half, "cuts")

    left_energy = from_left[2 * span :].reshape(-1)[:span]
    right_energy = from_right[2 * span :].reshape(-1)[:span]
    weight_left = jnp.concatenate([left_energy, energy])
    weight_diag = jnp.concatenate([left_energy, energy, right_energy])
    weight_right = jnp.concatenate([energy, right_energy])
    block_left = pair_block(full[: 2 * span], weight_left[:, None] * from_left[: 2 * span])
    block_diag = pair_block(full, weight_diag[:, None] * share)
    block_right = pair_block(full[span:], weight_right[:, None] * from_right[: 2 * span])
    owners = lax.axis_size("elem")
    stacked = jnp.stack([block_left, block_diag, block_right], axis=0)
    pieces = stacked.reshape(3, owners, width // owners, quarter).transpose(1, 0, 2, 3)
    return lax.all_to_all(pieces, "elem", split_axis=0, concat_axis=0, tiled=True)


def solution(mesh):
    in_specs = (
        P("elem", "cuts", None),
        P("elem", "cuts"),
        P("elem", None, None, None, "cuts"),
        P("elem", None),
        P("elem", None),
        P(),
    )
    out_specs = P(None, None, "elem", "cuts")
    return jax.shard_map(local, mesh=mesh, in_specs=in_specs, out_specs=out_specs, check_vma=False)
```

```python
import jax
import jax.numpy as jnp
from jax import lax
from jax.experimental import pallas as pl
from jax.experimental.pallas import tpu as pltpu
from jax.sharding import PartitionSpec as P


def passed_along(block, axis, distance):
    devices = range(lax.axis_size(axis))
    route = [((i - distance) % len(devices), i) for i in devices]
    return lax.ppermute(block, axis, route)


def swapped(block, axis, bit):
    devices = range(lax.axis_size(axis))
    return lax.ppermute(block, axis, [(i, i ^ bit) for i in devices])


def summed_columns(partial_value, axis, quarter):
    rows = partial_value.shape[0]
    size = lax.axis_size(axis)
    me = lax.axis_index(axis)
    pairs = partial_value.reshape(rows, size // 2, 2, quarter)
    odd = (me & 1) != 0
    keep = jnp.where(odd, pairs[:, :, 1], pairs[:, :, 0])
    send = jnp.where(odd, pairs[:, :, 0], pairs[:, :, 1])
    half = keep + swapped(send, axis, 1)
    bit = 2
    while bit < size:
        half = half + swapped(half, axis, bit)
        bit *= 2
    share = lax.dynamic_index_in_dim(half, me // 2, 1, keepdims=False)
    return half, share


def gathered_columns(half, axis):
    rows, count, quarter = half.shape
    odd = (lax.axis_index(axis) & 1) != 0
    other = swapped(half, axis, 1)
    low = jnp.where(odd, other, half)
    high = jnp.where(odd, half, other)
    return jnp.stack([low, high], axis=2).reshape(rows, count * 2 * quarter)


def coefficient_kernel(weight_ref, basis_ref, projector_ref, out_ref):
    step = pl.program_id(0)
    scaled = (basis_ref[...].astype(jnp.float32) * weight_ref[...]).astype(jnp.bfloat16)
    product = lax.dot_general(
        scaled, projector_ref[...], (((1,), (1,)), ((), ())), preferred_element_type=jnp.float32
    )

    @pl.when(step == 0)
    def _():
        out_ref[...] = product

    @pl.when(step > 0)
    def _():
        out_ref[...] += product


def partial_coefficients(flat_projectors, basis_t, weight):
    rows, points = flat_projectors.shape
    width = basis_t.shape[0]
    depth = min(points, 1024)
    transposed = pl.pallas_call(
        coefficient_kernel,
        out_shape=jax.ShapeDtypeStruct((width, rows), jnp.float32),
        grid=(points // depth,),
        in_specs=[
            pl.BlockSpec((1, depth), lambda k: (0, k)),
            pl.BlockSpec((width, depth), lambda k: (0, k)),
            pl.BlockSpec((rows, depth), lambda k: (0, k)),
        ],
        out_specs=pl.BlockSpec((width, rows), lambda k: (0, 0)),
        compiler_params=pltpu.CompilerParams(dimension_semantics=("arbitrary",)),
        cost_estimate=pl.CostEstimate(
            flops=2 * rows * points * width,
            bytes_accessed=2 * rows * points + 2 * points * width + 4 * points + 4 * rows * width,
            transcendentals=0,
        ),
    )(weight.reshape(1, points), basis_t, flat_projectors)
    return transposed.T


def pair_block(left, right):
    return jnp.einsum("ib,ic->bc", left, right, precision=lax.Precision.HIGHEST)


def local(basis, quad_weight, projectors, species, counts, gamma_table):
    width = basis.shape[2]
    groups, atoms, slots, points = projectors.shape[1:]
    span = atoms * slots
    quarter = width // lax.axis_size("cuts")
    partial_value = partial_coefficients(
        projectors[0].reshape(groups * span, points), basis[0].T, quad_weight[0]
    )
    onehot = (
        species[0][:, None] == jnp.arange(gamma_table.shape[0], dtype=jnp.int32)[None, :]
    ).astype(jnp.float32)
    table = jnp.dot(onehot, gamma_table, precision=lax.Precision.HIGHEST)
    active = (jnp.arange(slots, dtype=jnp.int32)[None, :] < counts[0][:, None]).astype(jnp.float32)
    energy = (table * active).reshape(span)

    half, share = summed_columns(partial_value, "cuts", quarter)
    energy_rows = -(-span // quarter)
    packed_energy = jnp.pad(energy, (0, energy_rows * quarter - span)).reshape(energy_rows, quarter)
    to_right = jnp.concatenate([share[span:], packed_energy], axis=0)
    to_left = jnp.concatenate([share[: 2 * span], packed_energy], axis=0)
    from_left = passed_along(to_right, "elem", 1)
    from_right = passed_along(to_left, "elem", -1)
    full = gathered_columns(half, "cuts")

    left_energy = from_left[2 * span :].reshape(-1)[:span]
    right_energy = from_right[2 * span :].reshape(-1)[:span]
    weight_left = jnp.concatenate([left_energy, energy])
    weight_diag = jnp.concatenate([left_energy, energy, right_energy])
    weight_right = jnp.concatenate([energy, right_energy])
    block_left = pair_block(full[: 2 * span], weight_left[:, None] * from_left[: 2 * span])
    block_diag = pair_block(full, weight_diag[:, None] * share)
    block_right = pair_block(full[span:], weight_right[:, None] * from_right[: 2 * span])
    owners = lax.axis_size("elem")
    stacked = jnp.stack([block_left, block_diag, block_right], axis=0)
    pieces = stacked.reshape(3, owners, width // owners, quarter).transpose(1, 0, 2, 3)
    return lax.all_to_all(pieces, "elem", split_axis=0, concat_axis=0, tiled=True)


def solution(mesh):
    in_specs = (
        P("elem", "cuts", None),
        P("elem", "cuts"),
        P("elem", None, None, None, "cuts"),
        P("elem", None),
        P("elem", None),
        P(),
    )
    out_specs = P(None, None, "elem", "cuts")
    return jax.shard_map(local, mesh=mesh, in_specs=in_specs, out_specs=out_specs, check_vma=False)
```

```python
import jax
import jax.numpy as jnp
from jax import lax
from jax.experimental import pallas as pl
from jax.experimental.pallas import tpu as pltpu
from jax.sharding import PartitionSpec as P


def passed_along(block, axis, distance):
    devices = range(lax.axis_size(axis))
    route = [((i - distance) % len(devices), i) for i in devices]
    return lax.ppermute(block, axis, route)


def swapped(block, axis, bit):
    devices = range(lax.axis_size(axis))
    return lax.ppermute(block, axis, [(i, i ^ bit) for i in devices])


def summed_rows(partial_t, axis, quarter):
    columns = partial_t.shape[1]
    size = lax.axis_size(axis)
    me = lax.axis_index(axis)
    pairs = partial_t.reshape(size // 2, 2, quarter, columns)
    odd = (me & 1) != 0
    keep = jnp.where(odd, pairs[:, 1], pairs[:, 0])
    send = jnp.where(odd, pairs[:, 0], pairs[:, 1])
    half = keep + swapped(send, axis, 1)
    bit = 2
    while bit < size:
        half = half + swapped(half, axis, bit)
        bit *= 2
    share = lax.dynamic_index_in_dim(half, me // 2, 0, keepdims=False)
    return half, share


def gathered_rows(half, axis):
    count, quarter, columns = half.shape
    odd = (lax.axis_index(axis) & 1) != 0
    other = swapped(half, axis, 1)
    low = jnp.where(odd, other, half)
    high = jnp.where(odd, half, other)
    return jnp.stack([low, high], axis=1).reshape(count * 2 * quarter, columns)


def coefficient_kernel(weight_ref, basis_ref, projector_ref, out_ref):
    step = pl.program_id(0)
    scaled = (basis_ref[...].astype(jnp.float32) * weight_ref[...]).astype(jnp.bfloat16)
    product = lax.dot_general(
        scaled, projector_ref[...], (((1,), (1,)), ((), ())), preferred_element_type=jnp.float32
    )

    @pl.when(step == 0)
    def _():
        out_ref[...] = product

    @pl.when(step > 0)
    def _():
        out_ref[...] += product


def partial_coefficients(flat_projectors, basis_t, weight):
    rows, points = flat_projectors.shape
    width = basis_t.shape[0]
    depth = min(points, 2048)
    transposed = pl.pallas_call(
        coefficient_kernel,
        out_shape=jax.ShapeDtypeStruct((width, rows), jnp.float32),
        grid=(points // depth,),
        in_specs=[
            pl.BlockSpec((1, depth), lambda k: (0, k)),
            pl.BlockSpec((width, depth), lambda k: (0, k)),
            pl.BlockSpec((rows, depth), lambda k: (0, k)),
        ],
        out_specs=pl.BlockSpec((width, rows), lambda k: (0, 0)),
        compiler_params=pltpu.CompilerParams(dimension_semantics=("arbitrary",)),
        cost_estimate=pl.CostEstimate(
            flops=2 * rows * points * width,
            bytes_accessed=2 * rows * points + 2 * points * width + 4 * points + 4 * rows * width,
            transcendentals=0,
        ),
    )(weight.reshape(1, points), basis_t, flat_projectors)
    return transposed


def pair_block(left_t, right_t):
    return lax.dot_general(
        left_t, right_t, (((1,), (1,)), ((), ())), precision=lax.Precision.HIGHEST
    )


def local(basis, quad_weight, projectors, species, counts, gamma_table):
    width = basis.shape[2]
    groups, atoms, slots, points = projectors.shape[1:]
    span = atoms * slots
    quarter = width // lax.axis_size("cuts")
    partial_t = partial_coefficients(
        projectors[0].reshape(groups * span, points), basis[0].T, quad_weight[0]
    )
    onehot = (
        species[0][:, None] == jnp.arange(gamma_table.shape[0], dtype=jnp.int32)[None, :]
    ).astype(jnp.float32)
    table = jnp.dot(onehot, gamma_table, precision=lax.Precision.HIGHEST)
    active = (jnp.arange(slots, dtype=jnp.int32)[None, :] < counts[0][:, None]).astype(jnp.float32)
    energy = (table * active).reshape(span)

    half, share = summed_rows(partial_t, "cuts", quarter)
    energy_row = jnp.pad(energy, (0, span))[None]
    to_right = jnp.concatenate([share[:, span:], energy_row], axis=0)
    to_left = jnp.concatenate([share[:, : 2 * span], energy_row], axis=0)
    from_left = passed_along(to_right, "elem", 1)
    from_right = passed_along(to_left, "elem", -1)
    full_t = gathered_rows(half, "cuts")

    left_energy = from_left[quarter, :span]
    right_energy = from_right[quarter, :span]
    weight_left = jnp.concatenate([left_energy, energy])
    weight_diag = jnp.concatenate([left_energy, energy, right_energy])
    weight_right = jnp.concatenate([energy, right_energy])
    block_left = pair_block(full_t[:, : 2 * span], from_left[:quarter] * weight_left[None])
    block_diag = pair_block(full_t, share * weight_diag[None])
    block_right = pair_block(full_t[:, span:], from_right[:quarter] * weight_right[None])
    owners = lax.axis_size("elem")
    stacked = jnp.stack([block_left, block_diag, block_right], axis=0)
    pieces = stacked.reshape(3, owners, width // owners, quarter).transpose(1, 0, 2, 3)
    return lax.all_to_all(pieces, "elem", split_axis=0, concat_axis=0, tiled=True)


def solution(mesh):
    in_specs = (
        P("elem", "cuts", None),
        P("elem", "cuts"),
        P("elem", None, None, None, "cuts"),
        P("elem", None),
        P("elem", None),
        P(),
    )
    out_specs = P(None, None, "elem", "cuts")
    return jax.shard_map(local, mesh=mesh, in_specs=in_specs, out_specs=out_specs, check_vma=False)
```

```python
import functools

import jax
import jax.numpy as jnp
from jax import lax
from jax.experimental import pallas as pl
from jax.experimental.pallas import tpu as pltpu
from jax.sharding import PartitionSpec as P


def passed_along(block, axis, distance):
    devices = range(lax.axis_size(axis))
    route = [((i - distance) % len(devices), i) for i in devices]
    return lax.ppermute(block, axis, route)


def swapped(block, axis, bit):
    devices = range(lax.axis_size(axis))
    return lax.ppermute(block, axis, [(i, i ^ bit) for i in devices])


def summed_rows(keep, send, axis):
    size = lax.axis_size(axis)
    me = lax.axis_index(axis)
    count = size // 2
    quarter = keep.shape[0] // count
    half = (keep + swapped(send, axis, 1)).reshape(count, quarter, keep.shape[1])
    mine = me // 2
    if count == 2:
        theirs = 1 - mine
        share = lax.dynamic_index_in_dim(half, mine, 0, keepdims=False) + swapped(
            lax.dynamic_index_in_dim(half, theirs, 0, keepdims=False), axis, 2
        )
        other = swapped(share, axis, 2)
        first = jnp.where(mine == 0, share, other)
        second = jnp.where(mine == 0, other, share)
        return jnp.stack([first, second]), share
    bit = 2
    while bit < size:
        half = half + swapped(half, axis, bit)
        bit *= 2
    return half, lax.dynamic_index_in_dim(half, mine, 0, keepdims=False)


def gathered_rows(half, axis):
    count, quarter, columns = half.shape
    odd = (lax.axis_index(axis) & 1) != 0
    other = swapped(half, axis, 1)
    low = jnp.where(odd, other, half)
    high = jnp.where(odd, half, other)
    return jnp.stack([low, high], axis=1).reshape(count * 2 * quarter, columns)


def coefficient_kernel(quarter, parity_ref, weight_ref, basis_ref, projector_ref, keep_ref, send_ref, total_ref):
    step = pl.program_id(0)
    scaled = (basis_ref[...].astype(jnp.float32) * weight_ref[...]).astype(jnp.bfloat16)
    product = lax.dot_general(
        scaled, projector_ref[...], (((1,), (1,)), ((), ())), preferred_element_type=jnp.float32
    )

    @pl.when(step == 0)
    def _():
        total_ref[...] = product

    @pl.when(step > 0)
    def _():
        total_ref[...] += product

    @pl.when(step == pl.num_programs(0) - 1)
    def _():
        count = keep_ref.shape[0] // quarter
        odd = parity_ref[0]
        for t in range(count):
            kept = pl.multiple_of((2 * t + odd) * quarter, 8)
            sent = pl.multiple_of((2 * t + 1 - odd) * quarter, 8)
            keep_ref[t * quarter : (t + 1) * quarter, :] = total_ref[pl.ds(kept, quarter), :]
            send_ref[t * quarter : (t + 1) * quarter, :] = total_ref[pl.ds(sent, quarter), :]


def partial_coefficients(flat_projectors, basis_t, weight, parity, quarter):
    rows, points = flat_projectors.shape
    width = basis_t.shape[0]
    depth = min(points, 4096)
    half = jax.ShapeDtypeStruct((width // 2, rows), jnp.float32)
    grid_spec = pltpu.PrefetchScalarGridSpec(
        num_scalar_prefetch=1,
        grid=(points // depth,),
        in_specs=[
            pl.BlockSpec((1, depth), lambda k, p: (0, k)),
            pl.BlockSpec((width, depth), lambda k, p: (0, k)),
            pl.BlockSpec((rows, depth), lambda k, p: (0, k)),
        ],
        out_specs=[
            pl.BlockSpec((width // 2, rows), lambda k, p: (0, 0)),
            pl.BlockSpec((width // 2, rows), lambda k, p: (0, 0)),
        ],
        scratch_shapes=[pltpu.VMEM((width, rows), jnp.float32)],
    )
    return pl.pallas_call(
        functools.partial(coefficient_kernel, quarter),
        out_shape=(half, half),
        grid_spec=grid_spec,
        compiler_params=pltpu.CompilerParams(dimension_semantics=("arbitrary",)),
        cost_estimate=pl.CostEstimate(
            flops=2 * rows * points * width,
            bytes_accessed=2 * rows * points + 2 * points * width + 4 * points + 4 * rows * width,
            transcendentals=0,
        ),
    )(parity, weight.reshape(1, points), basis_t, flat_projectors)


def pair_block(left_t, right_t):
    return lax.dot_general(
        left_t, right_t, (((1,), (1,)), ((), ())), precision=lax.Precision.HIGHEST
    )


def local(basis, quad_weight, projectors, species, counts, gamma_table):
    width = basis.shape[2]
    groups, atoms, slots, points = projectors.shape[1:]
    span = atoms * slots
    quarter = width // lax.axis_size("cuts")
    parity = (lax.axis_index("cuts") % 2).astype(jnp.int32).reshape(1)
    keep, send = partial_coefficients(
        projectors[0].reshape(groups * span, points), basis[0].T, quad_weight[0], parity, quarter
    )
    onehot = (
        species[0][:, None] == jnp.arange(gamma_table.shape[0], dtype=jnp.int32)[None, :]
    ).astype(jnp.float32)
    table = jnp.dot(onehot, gamma_table, precision=lax.Precision.HIGHEST)
    active = (jnp.arange(slots, dtype=jnp.int32)[None, :] < counts[0][:, None]).astype(jnp.float32)
    energy = (table * active).reshape(span)

    half, share = summed_rows(keep, send, "cuts")
    energy_row = jnp.pad(energy, (0, span))[None]
    to_right = jnp.concatenate([share[:, span:], energy_row], axis=0)
    to_left = jnp.concatenate([share[:, : 2 * span], energy_row], axis=0)
    from_left = passed_along(to_right, "elem", 1)
    from_right = passed_along(to_left, "elem", -1)
    full_t = gathered_rows(half, "cuts")

    left_energy = from_left[quarter, :span]
    right_energy = from_right[quarter, :span]
    weight_left = jnp.concatenate([left_energy, energy])
    weight_diag = jnp.concatenate([left_energy, energy, right_energy])
    weight_right = jnp.concatenate([energy, right_energy])
    block_left = pair_block(full_t[:, : 2 * span], from_left[:quarter] * weight_left[None])
    block_diag = pair_block(full_t, share * weight_diag[None])
    block_right = pair_block(full_t[:, span:], from_right[:quarter] * weight_right[None])
    owners = lax.axis_size("elem")
    stacked = jnp.stack([block_left, block_diag, block_right], axis=0)
    pieces = stacked.reshape(3, owners, width // owners, quarter).transpose(1, 0, 2, 3)
    return lax.all_to_all(pieces, "elem", split_axis=0, concat_axis=0, tiled=True)


def solution(mesh):
    in_specs = (
        P("elem", "cuts", None),
        P("elem", "cuts"),
        P("elem", None, None, None, "cuts"),
        P("elem", None),
        P("elem", None),
        P(),
    )
    out_specs = P(None, None, "elem", "cuts")
    return jax.shard_map(local, mesh=mesh, in_specs=in_specs, out_specs=out_specs, check_vma=False)
```

```python
import functools

import jax
import jax.numpy as jnp
from jax import lax
from jax.experimental import pallas as pl
from jax.experimental.pallas import tpu as pltpu
from jax.sharding import PartitionSpec as P


def passed_along(block, axis, distance):
    devices = range(lax.axis_size(axis))
    route = [((i - distance) % len(devices), i) for i in devices]
    return lax.ppermute(block, axis, route)


def swapped(block, axis, bit):
    devices = range(lax.axis_size(axis))
    return lax.ppermute(block, axis, [(i, i ^ bit) for i in devices])


def chip_reduced(keep, send, axis):
    size = lax.axis_size(axis)
    me = lax.axis_index(axis)
    count = size // 2
    quarter = keep.shape[0] // count
    half = (keep + swapped(send, axis, 1)).reshape(count, quarter, keep.shape[1])
    mine = me // 2
    if count == 2:
        share = lax.dynamic_index_in_dim(half, mine, 0, keepdims=False) + swapped(
            lax.dynamic_index_in_dim(half, 1 - mine, 0, keepdims=False), axis, 2
        )
        return share, None
    bit = 2
    while bit < size:
        half = half + swapped(half, axis, bit)
        bit *= 2
    return lax.dynamic_index_in_dim(half, mine, 0, keepdims=False), half


def chip_gathered(share, half, axis):
    if half is not None:
        return half
    first_here = (lax.axis_index(axis) // 2) == 0
    other = swapped(share, axis, 2)
    return jnp.stack([jnp.where(first_here, share, other), jnp.where(first_here, other, share)])


def gathered_rows(half, axis):
    count, quarter, columns = half.shape
    odd = (lax.axis_index(axis) & 1) != 0
    other = swapped(half, axis, 1)
    low = jnp.where(odd, other, half)
    high = jnp.where(odd, half, other)
    return jnp.stack([low, high], axis=1).reshape(count * 2 * quarter, columns)


def coefficient_kernel(quarter, parity_ref, weight_ref, basis_ref, projector_ref, keep_ref, send_ref, total_ref):
    step = pl.program_id(0)
    scaled = (basis_ref[...].astype(jnp.float32) * weight_ref[...]).astype(jnp.bfloat16)
    product = lax.dot_general(
        scaled, projector_ref[...], (((1,), (1,)), ((), ())), preferred_element_type=jnp.float32
    )

    @pl.when(step == 0)
    def _():
        total_ref[...] = product

    @pl.when(step > 0)
    def _():
        total_ref[...] += product

    @pl.when(step == pl.num_programs(0) - 1)
    def _():
        count = keep_ref.shape[0] // quarter
        odd = parity_ref[0]
        for t in range(count):
            kept = pl.multiple_of((2 * t + odd) * quarter, 8)
            sent = pl.multiple_of((2 * t + 1 - odd) * quarter, 8)
            keep_ref[t * quarter : (t + 1) * quarter, :] = total_ref[pl.ds(kept, quarter), :]
            send_ref[t * quarter : (t + 1) * quarter, :] = total_ref[pl.ds(sent, quarter), :]


def partial_coefficients(flat_projectors, basis_t, weight, parity, quarter, rows, row_index):
    points = flat_projectors.shape[1]
    width = basis_t.shape[0]
    depth = min(points, 4096)
    half = jax.ShapeDtypeStruct((width // 2, rows), jnp.float32)
    grid_spec = pltpu.PrefetchScalarGridSpec(
        num_scalar_prefetch=1,
        grid=(points // depth,),
        in_specs=[
            pl.BlockSpec((1, depth), lambda k, p: (0, k)),
            pl.BlockSpec((width, depth), lambda k, p: (0, k)),
            pl.BlockSpec((rows, depth), lambda k, p: (row_index, k)),
        ],
        out_specs=[
            pl.BlockSpec((width // 2, rows), lambda k, p: (0, 0)),
            pl.BlockSpec((width // 2, rows), lambda k, p: (0, 0)),
        ],
        scratch_shapes=[pltpu.VMEM((width, rows), jnp.float32)],
    )
    return pl.pallas_call(
        functools.partial(coefficient_kernel, quarter),
        out_shape=(half, half),
        grid_spec=grid_spec,
        compiler_params=pltpu.CompilerParams(dimension_semantics=("arbitrary",)),
        cost_estimate=pl.CostEstimate(
            flops=2 * rows * points * width,
            bytes_accessed=2 * rows * points + 2 * points * width + 4 * points + 4 * rows * width,
            transcendentals=0,
        ),
    )(parity, weight.reshape(1, points), basis_t, flat_projectors)


def pair_block(left_t, right_t):
    return lax.dot_general(
        left_t, right_t, (((1,), (1,)), ((), ())), precision=lax.Precision.HIGHEST
    )


def local(basis, quad_weight, projectors, species, counts, gamma_table):
    width = basis.shape[2]
    groups, atoms, slots, points = projectors.shape[1:]
    span = atoms * slots
    quarter = width // lax.axis_size("cuts")
    onehot = (
        species[0][:, None] == jnp.arange(gamma_table.shape[0], dtype=jnp.int32)[None, :]
    ).astype(jnp.float32)
    table = jnp.dot(onehot, gamma_table, precision=lax.Precision.HIGHEST)
    active = (jnp.arange(slots, dtype=jnp.int32)[None, :] < counts[0][:, None]).astype(jnp.float32)
    energy = (table * active).reshape(span)

    parity = (lax.axis_index("cuts") % 2).astype(jnp.int32).reshape(1)
    flat = projectors[0].reshape(groups * span, points)
    keep_first, send_first = partial_coefficients(
        flat, basis[0].T, quad_weight[0], parity, quarter, 2 * span, 0
    )
    keep_first, send_first, parity = lax.optimization_barrier((keep_first, send_first, parity))
    keep_last, send_last = partial_coefficients(
        flat, basis[0].T, quad_weight[0], parity, quarter, span, 2
    )
    share_first, half_first = chip_reduced(keep_first, send_first, "cuts")
    energy_row = jnp.pad(energy, (0, span))[None]
    to_left = jnp.concatenate([share_first, energy_row], axis=0)
    from_right = passed_along(to_left, "elem", -1)
    share_last, half_last = chip_reduced(keep_last, send_last, "cuts")
    share = jnp.concatenate([share_first, share_last], axis=1)
    to_right = jnp.concatenate([share[:, span:], energy_row], axis=0)
    from_left = passed_along(to_right, "elem", 1)
    half = None if half_first is None else jnp.concatenate([half_first, half_last], axis=2)
    full_t = gathered_rows(chip_gathered(share, half, "cuts"), "cuts")

    left_energy = from_left[quarter, :span]
    right_energy = from_right[quarter, :span]
    weight_left = jnp.concatenate([left_energy, energy])
    weight_diag = jnp.concatenate([left_energy, energy, right_energy])
    weight_right = jnp.concatenate([energy, right_energy])
    block_left = pair_block(full_t[:, : 2 * span], from_left[:quarter] * weight_left[None])
    block_diag = pair_block(full_t, share * weight_diag[None])
    block_right = pair_block(full_t[:, span:], from_right[:quarter] * weight_right[None])
    owners = lax.axis_size("elem")
    stacked = jnp.stack([block_left, block_diag, block_right], axis=0)
    pieces = stacked.reshape(3, owners, width // owners, quarter).transpose(1, 0, 2, 3)
    return lax.all_to_all(pieces, "elem", split_axis=0, concat_axis=0, tiled=True)


def solution(mesh):
    in_specs = (
        P("elem", "cuts", None),
        P("elem", "cuts"),
        P("elem", None, None, None, "cuts"),
        P("elem", None),
        P("elem", None),
        P(),
    )
    out_specs = P(None, None, "elem", "cuts")
    return jax.shard_map(local, mesh=mesh, in_specs=in_specs, out_specs=out_specs, check_vma=False)
```

```python
import functools

import jax
import jax.numpy as jnp
from jax import lax
from jax.experimental import pallas as pl
from jax.experimental.pallas import tpu as pltpu
from jax.sharding import PartitionSpec as P


def passed_along(block, axis, distance):
    devices = range(lax.axis_size(axis))
    route = [((i - distance) % len(devices), i) for i in devices]
    return lax.ppermute(block, axis, route)


def swapped(block, axis, bit):
    devices = range(lax.axis_size(axis))
    return lax.ppermute(block, axis, [(i, i ^ bit) for i in devices])


def summed_rows(keep, send, axis):
    size = lax.axis_size(axis)
    me = lax.axis_index(axis)
    count = size // 2
    quarter = keep.shape[0] // count
    mine = me // 2
    if count == 2:
        theirs = 1 - mine
        received = swapped(send, axis, 1).reshape(count, quarter, keep.shape[1])
        kept = keep.reshape(count, quarter, keep.shape[1])

        def summed(index):
            return lax.dynamic_index_in_dim(kept, index, 0, keepdims=False) + lax.dynamic_index_in_dim(
                received, index, 0, keepdims=False
            )

        share = summed(mine) + swapped(summed(theirs), axis, 2)
        other = swapped(share, axis, 2)
        first = jnp.where(mine == 0, share, other)
        second = jnp.where(mine == 0, other, share)
        return jnp.stack([first, second]), share
    half = (keep + swapped(send, axis, 1)).reshape(count, quarter, keep.shape[1])
    bit = 2
    while bit < size:
        half = half + swapped(half, axis, bit)
        bit *= 2
    return half, lax.dynamic_index_in_dim(half, mine, 0, keepdims=False)


def gathered_rows(half, axis):
    count, quarter, columns = half.shape
    odd = (lax.axis_index(axis) & 1) != 0
    other = swapped(half, axis, 1)
    low = jnp.where(odd, other, half)
    high = jnp.where(odd, half, other)
    return jnp.stack([low, high], axis=1).reshape(count * 2 * quarter, columns)


def coefficient_kernel(quarter, parity_ref, weight_ref, basis_ref, projector_ref, keep_ref, send_ref, total_ref):
    step = pl.program_id(0)
    scaled = (basis_ref[...].astype(jnp.float32) * weight_ref[...]).astype(jnp.bfloat16)
    product = lax.dot_general(
        scaled, projector_ref[...], (((1,), (1,)), ((), ())), preferred_element_type=jnp.float32
    )

    @pl.when(step == 0)
    def _():
        total_ref[...] = product

    @pl.when(step > 0)
    def _():
        total_ref[...] += product

    @pl.when(step == pl.num_programs(0) - 1)
    def _():
        count = keep_ref.shape[0] // quarter
        odd = parity_ref[0]
        for t in range(count):
            kept = pl.multiple_of((2 * t + odd) * quarter, 8)
            sent = pl.multiple_of((2 * t + 1 - odd) * quarter, 8)
            keep_ref[t * quarter : (t + 1) * quarter, :] = total_ref[pl.ds(kept, quarter), :]
            send_ref[t * quarter : (t + 1) * quarter, :] = total_ref[pl.ds(sent, quarter), :]


def partial_coefficients(flat_projectors, basis_t, weight, parity, quarter):
    rows, points = flat_projectors.shape
    width = basis_t.shape[0]
    depth = min(points, 4096)
    half = jax.ShapeDtypeStruct((width // 2, rows), jnp.float32)
    grid_spec = pltpu.PrefetchScalarGridSpec(
        num_scalar_prefetch=1,
        grid=(points // depth,),
        in_specs=[
            pl.BlockSpec((1, depth), lambda k, p: (0, k)),
            pl.BlockSpec((width, depth), lambda k, p: (0, k)),
            pl.BlockSpec((rows, depth), lambda k, p: (0, k)),
        ],
        out_specs=[
            pl.BlockSpec((width // 2, rows), lambda k, p: (0, 0)),
            pl.BlockSpec((width // 2, rows), lambda k, p: (0, 0)),
        ],
        scratch_shapes=[pltpu.VMEM((width, rows), jnp.float32)],
    )
    return pl.pallas_call(
        functools.partial(coefficient_kernel, quarter),
        out_shape=(half, half),
        grid_spec=grid_spec,
        compiler_params=pltpu.CompilerParams(dimension_semantics=("arbitrary",)),
        cost_estimate=pl.CostEstimate(
            flops=2 * rows * points * width,
            bytes_accessed=2 * rows * points + 2 * points * width + 4 * points + 4 * rows * width,
            transcendentals=0,
        ),
    )(parity, weight.reshape(1, points), basis_t, flat_projectors)


def pair_block(left_t, right_t):
    return lax.dot_general(
        left_t, right_t, (((1,), (1,)), ((), ())), precision=lax.Precision.HIGH
    )


def local(basis, quad_weight, projectors, species, counts, gamma_table):
    width = basis.shape[2]
    groups, atoms, slots, points = projectors.shape[1:]
    span = atoms * slots
    quarter = width // lax.axis_size("cuts")
    parity = (lax.axis_index("cuts") % 2).astype(jnp.int32).reshape(1)
    keep, send = partial_coefficients(
        projectors[0].reshape(groups * span, points), basis[0].T, quad_weight[0], parity, quarter
    )
    onehot = (
        species[0][:, None] == jnp.arange(gamma_table.shape[0], dtype=jnp.int32)[None, :]
    ).astype(jnp.float32)
    table = jnp.dot(onehot, gamma_table, precision=lax.Precision.HIGHEST)
    active = (jnp.arange(slots, dtype=jnp.int32)[None, :] < counts[0][:, None]).astype(jnp.float32)
    energy = (table * active).reshape(span)

    half, share = summed_rows(keep, send, "cuts")
    energy_row = jnp.pad(energy, (0, span))[None]
    to_right = jnp.concatenate([share[:, span:], energy_row], axis=0)
    to_left = jnp.concatenate([share[:, : 2 * span], energy_row], axis=0)
    from_left = passed_along(to_right, "elem", 1)
    from_right = passed_along(to_left, "elem", -1)
    full_t = gathered_rows(half, "cuts")

    left_energy = from_left[quarter, :span]
    right_energy = from_right[quarter, :span]
    weight_left = jnp.concatenate([left_energy, energy])
    weight_diag = jnp.concatenate([left_energy, energy, right_energy])
    weight_right = jnp.concatenate([energy, right_energy])
    block_left = pair_block(full_t[:, : 2 * span], from_left[:quarter] * weight_left[None])
    block_diag = pair_block(full_t, share * weight_diag[None])
    block_right = pair_block(full_t[:, span:], from_right[:quarter] * weight_right[None])
    owners = lax.axis_size("elem")
    stacked = jnp.stack([block_left, block_diag, block_right], axis=0)
    pieces = stacked.reshape(3, owners, width // owners, quarter).transpose(1, 0, 2, 3)
    return lax.all_to_all(pieces, "elem", split_axis=0, concat_axis=0, tiled=True)


def solution(mesh):
    in_specs = (
        P("elem", "cuts", None),
        P("elem", "cuts"),
        P("elem", None, None, None, "cuts"),
        P("elem", None),
        P("elem", None),
        P(),
    )
    out_specs = P(None, None, "elem", "cuts")
    return jax.shard_map(local, mesh=mesh, in_specs=in_specs, out_specs=out_specs, check_vma=False)
```

```python
import functools

import jax
import jax.numpy as jnp
from jax import lax
from jax.experimental import pallas as pl
from jax.experimental.pallas import tpu as pltpu
from jax.sharding import PartitionSpec as P


def passed_along(block, axis, distance):
    devices = range(lax.axis_size(axis))
    route = [((i - distance) % len(devices), i) for i in devices]
    return lax.ppermute(block, axis, route)


def swapped(block, axis, bit):
    devices = range(lax.axis_size(axis))
    return lax.ppermute(block, axis, [(i, i ^ bit) for i in devices])


def summed_rows(keep, send, axis):
    size = lax.axis_size(axis)
    me = lax.axis_index(axis)
    count = size // 2
    quarter = keep.shape[0] // count
    mine = me // 2
    if count == 2:
        theirs = 1 - mine
        received = swapped(send, axis, 1).reshape(count, quarter, keep.shape[1])
        kept = keep.reshape(count, quarter, keep.shape[1])

        def summed(index):
            return lax.dynamic_index_in_dim(kept, index, 0, keepdims=False) + lax.dynamic_index_in_dim(
                received, index, 0, keepdims=False
            )

        share = summed(mine) + swapped(summed(theirs), axis, 2)
        other = swapped(share, axis, 2)
        first = jnp.where(mine == 0, share, other)
        second = jnp.where(mine == 0, other, share)
        return jnp.stack([first, second]), share
    half = (keep + swapped(send, axis, 1)).reshape(count, quarter, keep.shape[1])
    bit = 2
    while bit < size:
        half = half + swapped(half, axis, bit)
        bit *= 2
    return half, lax.dynamic_index_in_dim(half, mine, 0, keepdims=False)


def gathered_rows(half, axis):
    count, quarter, columns = half.shape
    odd = (lax.axis_index(axis) & 1) != 0
    other = swapped(half, axis, 1)
    low = jnp.where(odd, other, half)
    high = jnp.where(odd, half, other)
    return jnp.stack([low, high], axis=1).reshape(count * 2 * quarter, columns)


def coefficient_kernel(quarter, parity_ref, weight_ref, basis_ref, projector_ref, keep_ref, send_ref, total_ref):
    step = pl.program_id(0)
    scaled = (basis_ref[...].astype(jnp.float32) * weight_ref[...]).astype(jnp.bfloat16)
    product = lax.dot_general(
        scaled, projector_ref[...], (((1,), (1,)), ((), ())), preferred_element_type=jnp.float32
    )

    @pl.when(step == 0)
    def _():
        total_ref[...] = product

    @pl.when(step > 0)
    def _():
        total_ref[...] += product

    @pl.when(step == pl.num_programs(0) - 1)
    def _():
        count = keep_ref.shape[0] // quarter
        odd = parity_ref[0]
        for t in range(count):
            kept = pl.multiple_of((2 * t + odd) * quarter, 8)
            sent = pl.multiple_of((2 * t + 1 - odd) * quarter, 8)
            keep_ref[t * quarter : (t + 1) * quarter, :] = total_ref[pl.ds(kept, quarter), :]
            send_ref[t * quarter : (t + 1) * quarter, :] = total_ref[pl.ds(sent, quarter), :]


def partial_coefficients(flat_projectors, basis_t, weight, parity, quarter):
    rows, points = flat_projectors.shape
    width = basis_t.shape[0]
    depth = min(points, 4096)
    half = jax.ShapeDtypeStruct((width // 2, rows), jnp.float32)
    grid_spec = pltpu.PrefetchScalarGridSpec(
        num_scalar_prefetch=1,
        grid=(points // depth,),
        in_specs=[
            pl.BlockSpec((1, depth), lambda k, p: (0, k)),
            pl.BlockSpec((width, depth), lambda k, p: (0, k)),
            pl.BlockSpec((rows, depth), lambda k, p: (0, k)),
        ],
        out_specs=[
            pl.BlockSpec((width // 2, rows), lambda k, p: (0, 0)),
            pl.BlockSpec((width // 2, rows), lambda k, p: (0, 0)),
        ],
        scratch_shapes=[pltpu.VMEM((width, rows), jnp.float32)],
    )
    return pl.pallas_call(
        functools.partial(coefficient_kernel, quarter),
        out_shape=(half, half),
        grid_spec=grid_spec,
        compiler_params=pltpu.CompilerParams(dimension_semantics=("arbitrary",)),
        cost_estimate=pl.CostEstimate(
            flops=2 * rows * points * width,
            bytes_accessed=2 * rows * points + 2 * points * width + 4 * points + 4 * rows * width,
            transcendentals=0,
        ),
    )(parity, weight.reshape(1, points), basis_t, flat_projectors)


def pair_block(left_t, right_t):
    return lax.dot_general(
        left_t, right_t, (((1,), (1,)), ((), ())), precision=lax.Precision.HIGH
    )


def local(basis, quad_weight, projectors, species, counts, gamma_table):
    width = basis.shape[2]
    groups, atoms, slots, points = projectors.shape[1:]
    span = atoms * slots
    quarter = width // lax.axis_size("cuts")
    parity = (lax.axis_index("cuts") % 2).astype(jnp.int32).reshape(1)
    keep, send = partial_coefficients(
        projectors[0].reshape(groups * span, points), basis[0].T, quad_weight[0], parity, quarter
    )
    onehot = (
        species[0][:, None] == jnp.arange(gamma_table.shape[0], dtype=jnp.int32)[None, :]
    ).astype(jnp.float32)
    table = jnp.dot(onehot, gamma_table, precision=lax.Precision.HIGHEST)
    active = (jnp.arange(slots, dtype=jnp.int32)[None, :] < counts[0][:, None]).astype(jnp.float32)
    energy = (table * active).reshape(span)

    half, share = summed_rows(keep, send, "cuts")
    energy_row = jnp.pad(energy, (0, span))[None]
    to_right = jnp.concatenate([share[:, span:], energy_row], axis=0)
    to_left = jnp.concatenate([share[:, : 2 * span], energy_row], axis=0)
    from_left = passed_along(to_right, "elem", 1)
    from_right = passed_along(to_left, "elem", -1)
    full_t = gathered_rows(half, "cuts")

    left_energy = from_left[quarter, :span]
    right_energy = from_right[quarter, :span]
    weight_left = jnp.concatenate([left_energy, energy])
    weight_diag = jnp.concatenate([left_energy, energy, right_energy])
    weight_right = jnp.concatenate([energy, right_energy])
    block_left = pair_block(full_t[:, : 2 * span], from_left[:quarter] * weight_left[None])
    block_diag = pair_block(full_t, share * weight_diag[None])
    block_right = pair_block(full_t[:, span:], from_right[:quarter] * weight_right[None])
    owners = lax.axis_size("elem")
    stacked = jnp.stack([block_left, block_diag, block_right], axis=0)
    pieces = stacked.reshape(3, owners, width // owners, quarter).transpose(1, 0, 2, 3)
    received = lax.all_to_all(pieces.reshape(owners, -1), "elem", split_axis=0, concat_axis=0, tiled=True)
    return received.reshape(pieces.shape)


def solution(mesh):
    in_specs = (
        P("elem", "cuts", None),
        P("elem", "cuts"),
        P("elem", None, None, None, "cuts"),
        P("elem", None),
        P("elem", None),
        P(),
    )
    out_specs = P(None, None, "elem", "cuts")
    return jax.shard_map(local, mesh=mesh, in_specs=in_specs, out_specs=out_specs, check_vma=False)
```

```python
import functools

import jax
import jax.numpy as jnp
from jax import lax
from jax.experimental import pallas as pl
from jax.experimental.pallas import tpu as pltpu
from jax.sharding import PartitionSpec as P


def passed_along(block, axis, distance):
    devices = range(lax.axis_size(axis))
    route = [((i - distance) % len(devices), i) for i in devices]
    return lax.ppermute(block, axis, route)


def swapped(block, axis, bit):
    devices = range(lax.axis_size(axis))
    return lax.ppermute(block, axis, [(i, i ^ bit) for i in devices])


def summed_rows(keep, send, axis):
    size = lax.axis_size(axis)
    me = lax.axis_index(axis)
    count = size // 2
    quarter = keep.shape[0] // count
    mine = me // 2
    if count == 2:
        received = swapped(send, axis, 1).reshape(count, quarter, keep.shape[1])
        kept = keep.reshape(count, quarter, keep.shape[1])
        share = (kept[0] + received[0]) + swapped(kept[1] + received[1], axis, 2)
        other = swapped(share, axis, 2)
        first = jnp.where(mine == 0, share, other)
        second = jnp.where(mine == 0, other, share)
        return jnp.stack([first, second]), share
    half = (keep + swapped(send, axis, 1)).reshape(count, quarter, keep.shape[1])
    bit = 2
    while bit < size:
        half = half + swapped(half, axis, bit)
        bit *= 2
    return half, lax.dynamic_index_in_dim(half, mine, 0, keepdims=False)


def gathered_rows(half, axis):
    count, quarter, columns = half.shape
    odd = (lax.axis_index(axis) & 1) != 0
    other = swapped(half, axis, 1)
    low = jnp.where(odd, other, half)
    high = jnp.where(odd, half, other)
    return jnp.stack([low, high], axis=1).reshape(count * 2 * quarter, columns)


def coefficient_kernel(quarter, parity_ref, weight_ref, basis_ref, projector_ref, keep_ref, send_ref, total_ref):
    step = pl.program_id(0)
    scaled = (basis_ref[...].astype(jnp.float32) * weight_ref[...]).astype(jnp.bfloat16)
    product = lax.dot_general(
        scaled, projector_ref[...], (((1,), (1,)), ((), ())), preferred_element_type=jnp.float32
    )

    @pl.when(step == 0)
    def _():
        total_ref[...] = product

    @pl.when(step > 0)
    def _():
        total_ref[...] += product

    @pl.when(step == pl.num_programs(0) - 1)
    def _():
        count = keep_ref.shape[0] // quarter
        odd = parity_ref[0]
        first = parity_ref[1]
        for t in range(count):
            kept = pl.multiple_of((2 * (t ^ first) + odd) * quarter, 8)
            sent = pl.multiple_of((2 * (t ^ first) + 1 - odd) * quarter, 8)
            keep_ref[t * quarter : (t + 1) * quarter, :] = total_ref[pl.ds(kept, quarter), :]
            send_ref[t * quarter : (t + 1) * quarter, :] = total_ref[pl.ds(sent, quarter), :]


def partial_coefficients(flat_projectors, basis_t, weight, parity, quarter):
    rows, points = flat_projectors.shape
    width = basis_t.shape[0]
    depth = min(points, 4096)
    half = jax.ShapeDtypeStruct((width // 2, rows), jnp.float32)
    grid_spec = pltpu.PrefetchScalarGridSpec(
        num_scalar_prefetch=1,
        grid=(points // depth,),
        in_specs=[
            pl.BlockSpec((1, depth), lambda k, p: (0, k)),
            pl.BlockSpec((width, depth), lambda k, p: (0, k)),
            pl.BlockSpec((rows, depth), lambda k, p: (0, k)),
        ],
        out_specs=[
            pl.BlockSpec((width // 2, rows), lambda k, p: (0, 0)),
            pl.BlockSpec((width // 2, rows), lambda k, p: (0, 0)),
        ],
        scratch_shapes=[pltpu.VMEM((width, rows), jnp.float32)],
    )
    return pl.pallas_call(
        functools.partial(coefficient_kernel, quarter),
        out_shape=(half, half),
        grid_spec=grid_spec,
        compiler_params=pltpu.CompilerParams(dimension_semantics=("arbitrary",)),
        cost_estimate=pl.CostEstimate(
            flops=2 * rows * points * width,
            bytes_accessed=2 * rows * points + 2 * points * width + 4 * points + 4 * rows * width,
            transcendentals=0,
        ),
    )(parity, weight.reshape(1, points), basis_t, flat_projectors)


def pair_block(left_t, right_t):
    return lax.dot_general(
        left_t, right_t, (((1,), (1,)), ((), ())), precision=lax.Precision.HIGH
    )


def local(basis, quad_weight, projectors, species, counts, gamma_table):
    width = basis.shape[2]
    groups, atoms, slots, points = projectors.shape[1:]
    span = atoms * slots
    quarter = width // lax.axis_size("cuts")
    cut = lax.axis_index("cuts")
    first = cut // 2 if lax.axis_size("cuts") == 4 else 0
    parity = jnp.stack([cut % 2, first]).astype(jnp.int32)
    keep, send = partial_coefficients(
        projectors[0].reshape(groups * span, points), basis[0].T, quad_weight[0], parity, quarter
    )
    onehot = (
        species[0][:, None] == jnp.arange(gamma_table.shape[0], dtype=jnp.int32)[None, :]
    ).astype(jnp.float32)
    table = jnp.dot(onehot, gamma_table, precision=lax.Precision.HIGHEST)
    active = (jnp.arange(slots, dtype=jnp.int32)[None, :] < counts[0][:, None]).astype(jnp.float32)
    energy = (table * active).reshape(span)

    half, share = summed_rows(keep, send, "cuts")
    energy_row = jnp.pad(energy, (0, span))[None]
    to_right = jnp.concatenate([share[:, span:], energy_row], axis=0)
    to_left = jnp.concatenate([share[:, : 2 * span], energy_row], axis=0)
    from_left = passed_along(to_right, "elem", 1)
    from_right = passed_along(to_left, "elem", -1)
    full_t = gathered_rows(half, "cuts")

    left_energy = from_left[quarter, :span]
    right_energy = from_right[quarter, :span]
    weight_left = jnp.concatenate([left_energy, energy])
    weight_diag = jnp.concatenate([left_energy, energy, right_energy])
    weight_right = jnp.concatenate([energy, right_energy])
    block_left = pair_block(full_t[:, : 2 * span], from_left[:quarter] * weight_left[None])
    block_diag = pair_block(full_t, share * weight_diag[None])
    block_right = pair_block(full_t[:, span:], from_right[:quarter] * weight_right[None])
    owners = lax.axis_size("elem")
    stacked = jnp.stack([block_left, block_diag, block_right], axis=0)
    pieces = stacked.reshape(3, owners, width // owners, quarter).transpose(1, 0, 2, 3)
    received = lax.all_to_all(pieces.reshape(owners, -1), "elem", split_axis=0, concat_axis=0, tiled=True)
    return received.reshape(pieces.shape)


def solution(mesh):
    in_specs = (
        P("elem", "cuts", None),
        P("elem", "cuts"),
        P("elem", None, None, None, "cuts"),
        P("elem", None),
        P("elem", None),
        P(),
    )
    out_specs = P(None, None, "elem", "cuts")
    return jax.shard_map(local, mesh=mesh, in_specs=in_specs, out_specs=out_specs, check_vma=False)
```

```python
import functools

import jax
import jax.numpy as jnp
from jax import lax
from jax.experimental import pallas as pl
from jax.experimental.pallas import tpu as pltpu
from jax.sharding import PartitionSpec as P


def passed_along(block, axis, distance):
    devices = range(lax.axis_size(axis))
    route = [((i - distance) % len(devices), i) for i in devices]
    return lax.ppermute(block, axis, route)


def swapped(block, axis, bit):
    devices = range(lax.axis_size(axis))
    return lax.ppermute(block, axis, [(i, i ^ bit) for i in devices])


def summed_rows(keep, send, axis):
    size = lax.axis_size(axis)
    me = lax.axis_index(axis)
    count = size // 2
    quarter = keep.shape[0] // count
    mine = me // 2
    if count == 2:
        theirs = 1 - mine
        received = swapped(send, axis, 1).reshape(count, quarter, keep.shape[1])
        kept = keep.reshape(count, quarter, keep.shape[1])

        def summed(index):
            return lax.dynamic_index_in_dim(kept, index, 0, keepdims=False) + lax.dynamic_index_in_dim(
                received, index, 0, keepdims=False
            )

        share = summed(mine) + swapped(summed(theirs), axis, 2)
        return None, share
    half = (keep + swapped(send, axis, 1)).reshape(count, quarter, keep.shape[1])
    bit = 2
    while bit < size:
        half = half + swapped(half, axis, bit)
        bit *= 2
    return half, lax.dynamic_index_in_dim(half, mine, 0, keepdims=False)


def gathered_rows(half, share, axis):
    if half is None:
        me = lax.axis_index(axis)
        odd = (me & 1) != 0
        high = (me // 2) != 0
        beside = swapped(share, axis, 1)
        across = swapped(share, axis, 2)
        relayed = swapped(across, axis, 1)
        here = jnp.stack([jnp.where(odd, beside, share), jnp.where(odd, share, beside)])
        there = jnp.stack([jnp.where(odd, relayed, across), jnp.where(odd, across, relayed)])
        return jnp.where(high, jnp.stack([there, here]), jnp.stack([here, there])).reshape(
            4 * share.shape[0], share.shape[1]
        )
    count, quarter, columns = half.shape
    odd = (lax.axis_index(axis) & 1) != 0
    other = swapped(half, axis, 1)
    low = jnp.where(odd, other, half)
    high = jnp.where(odd, half, other)
    return jnp.stack([low, high], axis=1).reshape(count * 2 * quarter, columns)


def coefficient_kernel(quarter, parity_ref, weight_ref, basis_ref, projector_ref, keep_ref, send_ref, total_ref):
    step = pl.program_id(0)
    scaled = (basis_ref[...].astype(jnp.float32) * weight_ref[...]).astype(jnp.bfloat16)
    product = lax.dot_general(
        scaled, projector_ref[...], (((1,), (1,)), ((), ())), preferred_element_type=jnp.float32
    )

    @pl.when(step == 0)
    def _():
        total_ref[...] = product

    @pl.when(step > 0)
    def _():
        total_ref[...] += product

    @pl.when(step == pl.num_programs(0) - 1)
    def _():
        count = keep_ref.shape[0] // quarter
        odd = parity_ref[0]
        for t in range(count):
            kept = pl.multiple_of((2 * t + odd) * quarter, 8)
            sent = pl.multiple_of((2 * t + 1 - odd) * quarter, 8)
            keep_ref[t * quarter : (t + 1) * quarter, :] = total_ref[pl.ds(kept, quarter), :]
            send_ref[t * quarter : (t + 1) * quarter, :] = total_ref[pl.ds(sent, quarter), :]


def partial_coefficients(flat_projectors, basis_t, weight, parity, quarter):
    rows, points = flat_projectors.shape
    width = basis_t.shape[0]
    depth = min(points, 4096)
    half = jax.ShapeDtypeStruct((width // 2, rows), jnp.float32)
    grid_spec = pltpu.PrefetchScalarGridSpec(
        num_scalar_prefetch=1,
        grid=(points // depth,),
        in_specs=[
            pl.BlockSpec((1, depth), lambda k, p: (0, k)),
            pl.BlockSpec((width, depth), lambda k, p: (0, k)),
            pl.BlockSpec((rows, depth), lambda k, p: (0, k)),
        ],
        out_specs=[
            pl.BlockSpec((width // 2, rows), lambda k, p: (0, 0)),
            pl.BlockSpec((width // 2, rows), lambda k, p: (0, 0)),
        ],
        scratch_shapes=[pltpu.VMEM((width, rows), jnp.float32)],
    )
    return pl.pallas_call(
        functools.partial(coefficient_kernel, quarter),
        out_shape=(half, half),
        grid_spec=grid_spec,
        compiler_params=pltpu.CompilerParams(dimension_semantics=("arbitrary",)),
        cost_estimate=pl.CostEstimate(
            flops=2 * rows * points * width,
            bytes_accessed=2 * rows * points + 2 * points * width + 4 * points + 4 * rows * width,
            transcendentals=0,
        ),
    )(parity, weight.reshape(1, points), basis_t, flat_projectors)


def pair_block(left_t, right_t):
    return lax.dot_general(
        left_t, right_t, (((1,), (1,)), ((), ())), precision=lax.Precision.HIGH
    )


def local(basis, quad_weight, projectors, species, counts, gamma_table):
    width = basis.shape[2]
    groups, atoms, slots, points = projectors.shape[1:]
    span = atoms * slots
    quarter = width // lax.axis_size("cuts")
    parity = (lax.axis_index("cuts") % 2).astype(jnp.int32).reshape(1)
    keep, send = partial_coefficients(
        projectors[0].reshape(groups * span, points), basis[0].T, quad_weight[0], parity, quarter
    )
    onehot = (
        species[0][:, None] == jnp.arange(gamma_table.shape[0], dtype=jnp.int32)[None, :]
    ).astype(jnp.float32)
    table = jnp.dot(onehot, gamma_table, precision=lax.Precision.HIGHEST)
    active = (jnp.arange(slots, dtype=jnp.int32)[None, :] < counts[0][:, None]).astype(jnp.float32)
    energy = (table * active).reshape(span)

    half, share = summed_rows(keep, send, "cuts")
    energy_row = jnp.pad(energy, (0, span))[None]
    to_right = jnp.concatenate([share[:, span:], energy_row], axis=0)
    to_left = jnp.concatenate([share[:, : 2 * span], energy_row], axis=0)
    from_left = passed_along(to_right, "elem", 1)
    from_right = passed_along(to_left, "elem", -1)
    full_t = gathered_rows(half, share, "cuts")

    left_energy = from_left[quarter, :span]
    right_energy = from_right[quarter, :span]
    weight_left = jnp.concatenate([left_energy, energy])
    weight_diag = jnp.concatenate([left_energy, energy, right_energy])
    weight_right = jnp.concatenate([energy, right_energy])
    block_left = pair_block(full_t[:, : 2 * span], from_left[:quarter] * weight_left[None])
    block_diag = pair_block(full_t, share * weight_diag[None])
    block_right = pair_block(full_t[:, span:], from_right[:quarter] * weight_right[None])
    owners = lax.axis_size("elem")
    stacked = jnp.stack([block_left, block_diag, block_right], axis=0)
    pieces = stacked.reshape(3, owners, width // owners, quarter).transpose(1, 0, 2, 3)
    received = lax.all_to_all(pieces.reshape(owners, -1), "elem", split_axis=0, concat_axis=0, tiled=True)
    return received.reshape(pieces.shape)


def solution(mesh):
    in_specs = (
        P("elem", "cuts", None),
        P("elem", "cuts"),
        P("elem", None, None, None, "cuts"),
        P("elem", None),
        P("elem", None),
        P(),
    )
    out_specs = P(None, None, "elem", "cuts")
    return jax.shard_map(local, mesh=mesh, in_specs=in_specs, out_specs=out_specs, check_vma=False)
```

```python
import functools

import jax
import jax.numpy as jnp
from jax import lax
from jax.experimental import pallas as pl
from jax.experimental.pallas import tpu as pltpu
from jax.sharding import PartitionSpec as P


def passed_along(block, axis, distance):
    devices = range(lax.axis_size(axis))
    route = [((i - distance) % len(devices), i) for i in devices]
    return lax.ppermute(block, axis, route)


def swapped(block, axis, bit):
    devices = range(lax.axis_size(axis))
    return lax.ppermute(block, axis, [(i, i ^ bit) for i in devices])


def summed_rows(keep, send, axis):
    size = lax.axis_size(axis)
    me = lax.axis_index(axis)
    count = size // 2
    quarter = keep.shape[0] // count
    mine = me // 2
    if count == 2:
        theirs = 1 - mine
        received = swapped(send, axis, 1).reshape(count, quarter, keep.shape[1])
        kept = keep.reshape(count, quarter, keep.shape[1])

        def summed(index):
            return lax.dynamic_index_in_dim(kept, index, 0, keepdims=False) + lax.dynamic_index_in_dim(
                received, index, 0, keepdims=False
            )

        share = summed(mine) + swapped(summed(theirs), axis, 2)
        other = swapped(share, axis, 2)
        first = jnp.where(mine == 0, share, other)
        second = jnp.where(mine == 0, other, share)
        return jnp.stack([first, second]), share
    half = (keep + swapped(send, axis, 1)).reshape(count, quarter, keep.shape[1])
    bit = 2
    while bit < size:
        half = half + swapped(half, axis, bit)
        bit *= 2
    return half, lax.dynamic_index_in_dim(half, mine, 0, keepdims=False)


def gathered_rows(half, axis):
    count, quarter, columns = half.shape
    odd = (lax.axis_index(axis) & 1) != 0
    other = swapped(half, axis, 1)
    low = jnp.where(odd, other, half)
    high = jnp.where(odd, half, other)
    return jnp.stack([low, high], axis=1).reshape(count * 2 * quarter, columns)


def coefficient_kernel(quarter, parity_ref, weight_ref, basis_ref, projector_ref, keep_ref, send_ref, total_ref):
    step = pl.program_id(0)
    scaled = (basis_ref[...].astype(jnp.float32) * weight_ref[...]).astype(jnp.bfloat16)
    product = lax.dot_general(
        scaled, projector_ref[...], (((1,), (1,)), ((), ())), preferred_element_type=jnp.float32
    )

    @pl.when(step == 0)
    def _():
        total_ref[...] = product

    @pl.when(step > 0)
    def _():
        total_ref[...] += product

    @pl.when(step == pl.num_programs(0) - 1)
    def _():
        count = keep_ref.shape[0] // quarter
        odd = parity_ref[0]
        for t in range(count):
            kept = pl.multiple_of((2 * t + odd) * quarter, 8)
            sent = pl.multiple_of((2 * t + 1 - odd) * quarter, 8)
            keep_ref[t * quarter : (t + 1) * quarter, :] = total_ref[pl.ds(kept, quarter), :]
            send_ref[t * quarter : (t + 1) * quarter, :] = total_ref[pl.ds(sent, quarter), :]


def partial_coefficients(flat_projectors, basis_t, weight, parity, quarter):
    rows, points = flat_projectors.shape
    width = basis_t.shape[0]
    depth = min(points, 4096)
    half = jax.ShapeDtypeStruct((width // 2, rows), jnp.float32)
    grid_spec = pltpu.PrefetchScalarGridSpec(
        num_scalar_prefetch=1,
        grid=(points // depth,),
        in_specs=[
            pl.BlockSpec((1, depth), lambda k, p: (0, k)),
            pl.BlockSpec((width, depth), lambda k, p: (0, k)),
            pl.BlockSpec((rows, depth), lambda k, p: (0, k)),
        ],
        out_specs=[
            pl.BlockSpec((width // 2, rows), lambda k, p: (0, 0)),
            pl.BlockSpec((width // 2, rows), lambda k, p: (0, 0)),
        ],
        scratch_shapes=[pltpu.VMEM((width, rows), jnp.float32)],
    )
    return pl.pallas_call(
        functools.partial(coefficient_kernel, quarter),
        out_shape=(half, half),
        grid_spec=grid_spec,
        compiler_params=pltpu.CompilerParams(dimension_semantics=("arbitrary",)),
        cost_estimate=pl.CostEstimate(
            flops=2 * rows * points * width,
            bytes_accessed=2 * rows * points + 2 * points * width + 4 * points + 4 * rows * width,
            transcendentals=0,
        ),
    )(parity, weight.reshape(1, points), basis_t, flat_projectors)


def pair_block(left_t, right_t):
    return lax.dot_general(
        left_t, right_t, (((1,), (1,)), ((), ())), precision=lax.Precision.HIGH
    )


def local(basis, quad_weight, projectors, species, counts, gamma_table):
    width = basis.shape[2]
    groups, atoms, slots, points = projectors.shape[1:]
    span = atoms * slots
    quarter = width // lax.axis_size("cuts")
    parity = (lax.axis_index("cuts") % 2).astype(jnp.int32).reshape(1)
    keep, send = partial_coefficients(
        projectors[0].reshape(groups * span, points), basis[0].T, quad_weight[0], parity, quarter
    )
    onehot = (
        species[0][:, None] == jnp.arange(gamma_table.shape[0], dtype=jnp.int32)[None, :]
    ).astype(jnp.float32)
    table = jnp.dot(onehot, gamma_table, precision=lax.Precision.HIGHEST)
    active = (jnp.arange(slots, dtype=jnp.int32)[None, :] < counts[0][:, None]).astype(jnp.float32)
    energy = (table * active).reshape(span)

    half, share = summed_rows(keep, send, "cuts")
    energy_row = jnp.pad(energy, (0, span))[None]
    to_right = jnp.concatenate([share[:, span:], energy_row], axis=0)
    to_left = jnp.concatenate([share[:, : 2 * span], energy_row], axis=0)
    from_left = passed_along(to_right, "elem", 1)
    from_right = passed_along(to_left, "elem", -1)
    full_t = gathered_rows(half, "cuts")

    left_energy = from_left[quarter, :span]
    right_energy = from_right[quarter, :span]
    weight_left = jnp.concatenate([left_energy, energy])
    weight_diag = jnp.concatenate([left_energy, energy, right_energy])
    weight_right = jnp.concatenate([energy, right_energy])
    gap = jnp.zeros((quarter, span), jnp.float32)
    right_t = jnp.concatenate(
        [
            jnp.concatenate([from_left[:quarter] * weight_left[None], gap], axis=1),
            share * weight_diag[None],
            jnp.concatenate([gap, from_right[:quarter] * weight_right[None]], axis=1),
        ],
        axis=0,
    )
    owners = lax.axis_size("elem")
    stacked = pair_block(full_t, right_t).reshape(owners, width // owners, 3, quarter)
    pieces = stacked.transpose(0, 2, 1, 3)
    received = lax.all_to_all(pieces.reshape(owners, -1), "elem", split_axis=0, concat_axis=0, tiled=True)
    return received.reshape(pieces.shape)


def solution(mesh):
    in_specs = (
        P("elem", "cuts", None),
        P("elem", "cuts"),
        P("elem", None, None, None, "cuts"),
        P("elem", None),
        P("elem", None),
        P(),
    )
    out_specs = P(None, None, "elem", "cuts")
    return jax.shard_map(local, mesh=mesh, in_specs=in_specs, out_specs=out_specs, check_vma=False)
```

```python
import functools

import jax
import jax.numpy as jnp
from jax import lax
from jax.experimental import pallas as pl
from jax.experimental.pallas import tpu as pltpu
from jax.sharding import PartitionSpec as P


def passed_along(block, axis, distance):
    devices = range(lax.axis_size(axis))
    route = [((i - distance) % len(devices), i) for i in devices]
    return lax.ppermute(block, axis, route)


def swapped(block, axis, bit):
    devices = range(lax.axis_size(axis))
    return lax.ppermute(block, axis, [(i, i ^ bit) for i in devices])


def summed_rows(pieces, axis):
    share = pieces[0]
    for distance in range(1, pieces.shape[0]):
        share = share + swapped(pieces[distance], axis, distance)
    return share


def gathered_rows(share, axis):
    quarter, columns = share.shape
    size = lax.axis_size(axis)
    me = lax.axis_index(axis)
    held = share[None]
    bit = size // 2
    while bit >= 1:
        other = swapped(held, axis, bit)
        mine = (me & bit) != 0
        low = jnp.where(mine, other, held)
        high = jnp.where(mine, held, other)
        held = jnp.stack([low, high], axis=1).reshape(held.shape[0] * 2, quarter, columns)
        bit //= 2
    return held.reshape(size * quarter, columns)


def coefficient_kernel(quarter, cut_ref, weight_ref, basis_ref, projector_ref, pieces_ref, total_ref):
    step = pl.program_id(0)
    scaled = (basis_ref[...].astype(jnp.float32) * weight_ref[...]).astype(jnp.bfloat16)
    product = lax.dot_general(
        scaled, projector_ref[...], (((1,), (1,)), ((), ())), preferred_element_type=jnp.float32
    )

    @pl.when(step == 0)
    def _():
        total_ref[...] = product

    @pl.when(step > 0)
    def _():
        total_ref[...] += product

    @pl.when(step == pl.num_programs(0) - 1)
    def _():
        me = cut_ref[0]
        for distance in range(pieces_ref.shape[0]):
            start = pl.multiple_of((me ^ distance) * quarter, 8)
            pieces_ref[distance] = total_ref[pl.ds(start, quarter), :]


def partial_coefficients(flat_projectors, basis_t, weight, cut, quarter):
    rows, points = flat_projectors.shape
    width = basis_t.shape[0]
    depth = min(points, 4096)
    size = width // quarter
    grid_spec = pltpu.PrefetchScalarGridSpec(
        num_scalar_prefetch=1,
        grid=(points // depth,),
        in_specs=[
            pl.BlockSpec((1, depth), lambda k, p: (0, k)),
            pl.BlockSpec((width, depth), lambda k, p: (0, k)),
            pl.BlockSpec((rows, depth), lambda k, p: (0, k)),
        ],
        out_specs=pl.BlockSpec((size, quarter, rows), lambda k, p: (0, 0, 0)),
        scratch_shapes=[pltpu.VMEM((width, rows), jnp.float32)],
    )
    return pl.pallas_call(
        functools.partial(coefficient_kernel, quarter),
        out_shape=jax.ShapeDtypeStruct((size, quarter, rows), jnp.float32),
        grid_spec=grid_spec,
        compiler_params=pltpu.CompilerParams(dimension_semantics=("arbitrary",)),
        cost_estimate=pl.CostEstimate(
            flops=2 * rows * points * width,
            bytes_accessed=2 * rows * points + 2 * points * width + 4 * points + 4 * rows * width,
            transcendentals=0,
        ),
    )(cut, weight.reshape(1, points), basis_t, flat_projectors)


def pair_block(left_t, right_t):
    return lax.dot_general(
        left_t, right_t, (((1,), (1,)), ((), ())), precision=lax.Precision.HIGH
    )


def local(basis, quad_weight, projectors, species, counts, gamma_table):
    width = basis.shape[2]
    groups, atoms, slots, points = projectors.shape[1:]
    span = atoms * slots
    quarter = width // lax.axis_size("cuts")
    cut = lax.axis_index("cuts").astype(jnp.int32).reshape(1)
    pieces = partial_coefficients(
        projectors[0].reshape(groups * span, points), basis[0].T, quad_weight[0], cut, quarter
    )
    onehot = (
        species[0][:, None] == jnp.arange(gamma_table.shape[0], dtype=jnp.int32)[None, :]
    ).astype(jnp.float32)
    table = jnp.dot(onehot, gamma_table, precision=lax.Precision.HIGHEST)
    active = (jnp.arange(slots, dtype=jnp.int32)[None, :] < counts[0][:, None]).astype(jnp.float32)
    energy = (table * active).reshape(span)

    share = summed_rows(pieces, "cuts")
    energy_row = jnp.pad(energy, (0, span))[None]
    to_right = jnp.concatenate([share[:, span:], energy_row], axis=0)
    to_left = jnp.concatenate([share[:, : 2 * span], energy_row], axis=0)
    from_left = passed_along(to_right, "elem", 1)
    from_right = passed_along(to_left, "elem", -1)
    full_t = gathered_rows(share, "cuts")

    left_energy = from_left[quarter, :span]
    right_energy = from_right[quarter, :span]
    weight_left = jnp.concatenate([left_energy, energy])
    weight_diag = jnp.concatenate([left_energy, energy, right_energy])
    weight_right = jnp.concatenate([energy, right_energy])
    block_left = pair_block(full_t[:, : 2 * span], from_left[:quarter] * weight_left[None])
    block_diag = pair_block(full_t, share * weight_diag[None])
    block_right = pair_block(full_t[:, span:], from_right[:quarter] * weight_right[None])
    owners = lax.axis_size("elem")
    stacked = jnp.stack([block_left, block_diag, block_right], axis=0)
    pieces = stacked.reshape(3, owners, width // owners, quarter).transpose(1, 0, 2, 3)
    received = lax.all_to_all(pieces.reshape(owners, -1), "elem", split_axis=0, concat_axis=0, tiled=True)
    return received.reshape(pieces.shape)


def solution(mesh):
    in_specs = (
        P("elem", "cuts", None),
        P("elem", "cuts"),
        P("elem", None, None, None, "cuts"),
        P("elem", None),
        P("elem", None),
        P(),
    )
    out_specs = P(None, None, "elem", "cuts")
    return jax.shard_map(local, mesh=mesh, in_specs=in_specs, out_specs=out_specs, check_vma=False)
```

```python
import functools

import jax
import jax.numpy as jnp
from jax import lax
from jax.experimental import pallas as pl
from jax.experimental.pallas import tpu as pltpu
from jax.sharding import PartitionSpec as P


def passed_along(block, axis, distance):
    devices = range(lax.axis_size(axis))
    route = [((i - distance) % len(devices), i) for i in devices]
    return lax.ppermute(block, axis, route)


def swapped(block, axis, bit):
    devices = range(lax.axis_size(axis))
    return lax.ppermute(block, axis, [(i, i ^ bit) for i in devices])


def summed_rows(keep, send, axis):
    size = lax.axis_size(axis)
    me = lax.axis_index(axis)
    count = size // 2
    quarter = keep.shape[0] // count
    mine = me // 2
    if count == 2:
        theirs = 1 - mine
        received = swapped(send, axis, 1).reshape(count, quarter, keep.shape[1])
        kept = keep.reshape(count, quarter, keep.shape[1])

        def summed(index):
            return lax.dynamic_index_in_dim(kept, index, 0, keepdims=False) + lax.dynamic_index_in_dim(
                received, index, 0, keepdims=False
            )

        share = summed(mine) + swapped(summed(theirs), axis, 2)
        other = swapped(share, axis, 2)
        first = jnp.where(mine == 0, share, other)
        second = jnp.where(mine == 0, other, share)
        return jnp.stack([first, second]), share
    half = (keep + swapped(send, axis, 1)).reshape(count, quarter, keep.shape[1])
    bit = 2
    while bit < size:
        half = half + swapped(half, axis, bit)
        bit *= 2
    return half, lax.dynamic_index_in_dim(half, mine, 0, keepdims=False)


def gathered_rows(half, axis):
    count, quarter, columns = half.shape
    odd = (lax.axis_index(axis) & 1) != 0
    other = swapped(half, axis, 1)
    low = jnp.where(odd, other, half)
    high = jnp.where(odd, half, other)
    return jnp.stack([low, high], axis=1).reshape(count * 2 * quarter, columns)


def coefficient_kernel(
    quarter, chunk, parity_ref, weight_ref, basis_hbm, projector_hbm, keep_ref, send_ref,
    basis_buf, projector_buf, copies, total_ref,
):
    points = projector_hbm.shape[1]
    chunks = points // chunk
    slots = basis_buf.shape[0]

    def fetch(index):
        slot = index % slots
        window = pl.ds(index * chunk, chunk)
        return (
            pltpu.make_async_copy(basis_hbm.at[:, window], basis_buf.at[slot], copies.at[0, slot]),
            pltpu.make_async_copy(projector_hbm.at[:, window], projector_buf.at[slot], copies.at[1, slot]),
        )

    pending = {}
    for index in range(min(slots, chunks)):
        pending[index] = fetch(index)
        for copy in pending[index]:
            copy.start()
    for index in range(chunks):
        slot = index % slots
        for copy in pending.pop(index):
            copy.wait()
        weight = weight_ref[:, index * chunk : (index + 1) * chunk]
        scaled = (basis_buf[slot].astype(jnp.float32) * weight).astype(jnp.bfloat16)
        product = lax.dot_general(
            scaled, projector_buf[slot], (((1,), (1,)), ((), ())), preferred_element_type=jnp.float32
        )
        if index == 0:
            total_ref[...] = product
        else:
            total_ref[...] += product
        if index + slots < chunks:
            pending[index + slots] = fetch(index + slots)
            for copy in pending[index + slots]:
                copy.start()

    count = keep_ref.shape[0] // quarter
    odd = parity_ref[0]
    for t in range(count):
        kept = pl.multiple_of((2 * t + odd) * quarter, 8)
        sent = pl.multiple_of((2 * t + 1 - odd) * quarter, 8)
        keep_ref[t * quarter : (t + 1) * quarter, :] = total_ref[pl.ds(kept, quarter), :]
        send_ref[t * quarter : (t + 1) * quarter, :] = total_ref[pl.ds(sent, quarter), :]


def partial_coefficients(flat_projectors, basis_t, weight, parity, quarter):
    rows, points = flat_projectors.shape
    width = basis_t.shape[0]
    chunk = min(points, 1024)
    slots = 3
    half = jax.ShapeDtypeStruct((width // 2, rows), jnp.float32)
    grid_spec = pltpu.PrefetchScalarGridSpec(
        num_scalar_prefetch=1,
        grid=(1,),
        in_specs=[
            pl.BlockSpec((1, points), lambda k, p: (0, 0)),
            pl.BlockSpec(memory_space=pl.ANY),
            pl.BlockSpec(memory_space=pl.ANY),
        ],
        out_specs=[
            pl.BlockSpec((width // 2, rows), lambda k, p: (0, 0)),
            pl.BlockSpec((width // 2, rows), lambda k, p: (0, 0)),
        ],
        scratch_shapes=[
            pltpu.VMEM((slots, width, chunk), basis_t.dtype),
            pltpu.VMEM((slots, rows, chunk), flat_projectors.dtype),
            pltpu.SemaphoreType.DMA((2, slots)),
            pltpu.VMEM((width, rows), jnp.float32),
        ],
    )
    return pl.pallas_call(
        functools.partial(coefficient_kernel, quarter, chunk),
        out_shape=(half, half),
        grid_spec=grid_spec,
        compiler_params=pltpu.CompilerParams(dimension_semantics=("arbitrary",)),
        cost_estimate=pl.CostEstimate(
            flops=2 * rows * points * width,
            bytes_accessed=2 * rows * points + 2 * points * width + 4 * points + 4 * rows * width,
            transcendentals=0,
        ),
    )(parity, weight.reshape(1, points), basis_t, flat_projectors)


def pair_block(left_t, right_t):
    return lax.dot_general(
        left_t, right_t, (((1,), (1,)), ((), ())), precision=lax.Precision.HIGH
    )


def local(basis, quad_weight, projectors, species, counts, gamma_table):
    width = basis.shape[2]
    groups, atoms, slots, points = projectors.shape[1:]
    span = atoms * slots
    quarter = width // lax.axis_size("cuts")
    parity = (lax.axis_index("cuts") % 2).astype(jnp.int32).reshape(1)
    keep, send = partial_coefficients(
        projectors[0].reshape(groups * span, points), basis[0].T, quad_weight[0], parity, quarter
    )
    onehot = (
        species[0][:, None] == jnp.arange(gamma_table.shape[0], dtype=jnp.int32)[None, :]
    ).astype(jnp.float32)
    table = jnp.dot(onehot, gamma_table, precision=lax.Precision.HIGHEST)
    active = (jnp.arange(slots, dtype=jnp.int32)[None, :] < counts[0][:, None]).astype(jnp.float32)
    energy = (table * active).reshape(span)

    half, share = summed_rows(keep, send, "cuts")
    energy_row = jnp.pad(energy, (0, span))[None]
    to_right = jnp.concatenate([share[:, span:], energy_row], axis=0)
    to_left = jnp.concatenate([share[:, : 2 * span], energy_row], axis=0)
    from_left = passed_along(to_right, "elem", 1)
    from_right = passed_along(to_left, "elem", -1)
    full_t = gathered_rows(half, "cuts")

    left_energy = from_left[quarter, :span]
    right_energy = from_right[quarter, :span]
    weight_left = jnp.concatenate([left_energy, energy])
    weight_diag = jnp.concatenate([left_energy, energy, right_energy])
    weight_right = jnp.concatenate([energy, right_energy])
    block_left = pair_block(full_t[:, : 2 * span], from_left[:quarter] * weight_left[None])
    block_diag = pair_block(full_t, share * weight_diag[None])
    block_right = pair_block(full_t[:, span:], from_right[:quarter] * weight_right[None])
    owners = lax.axis_size("elem")
    stacked = jnp.stack([block_left, block_diag, block_right], axis=0)
    pieces = stacked.reshape(3, owners, width // owners, quarter).transpose(1, 0, 2, 3)
    received = lax.all_to_all(pieces.reshape(owners, -1), "elem", split_axis=0, concat_axis=0, tiled=True)
    return received.reshape(pieces.shape)


def solution(mesh):
    in_specs = (
        P("elem", "cuts", None),
        P("elem", "cuts"),
        P("elem", None, None, None, "cuts"),
        P("elem", None),
        P("elem", None),
        P(),
    )
    out_specs = P(None, None, "elem", "cuts")
    return jax.shard_map(local, mesh=mesh, in_specs=in_specs, out_specs=out_specs, check_vma=False)
```

```python
import functools

import jax
import jax.numpy as jnp
from jax import lax
from jax.experimental import pallas as pl
from jax.experimental.pallas import tpu as pltpu
from jax.sharding import PartitionSpec as P


def passed_along(block, axis, distance):
    devices = range(lax.axis_size(axis))
    route = [((i - distance) % len(devices), i) for i in devices]
    return lax.ppermute(block, axis, route)


def swapped(block, axis, bit):
    devices = range(lax.axis_size(axis))
    return lax.ppermute(block, axis, [(i, i ^ bit) for i in devices])


def summed_rows(keep, send, axis):
    size = lax.axis_size(axis)
    me = lax.axis_index(axis)
    count = size // 2
    quarter = keep.shape[0] // count
    mine = me // 2
    if count == 2:
        theirs = 1 - mine
        half = (keep + swapped(send, axis, 1)).reshape(count, quarter, keep.shape[1])
        share = lax.dynamic_index_in_dim(half, mine, 0, keepdims=False) + swapped(
            lax.dynamic_index_in_dim(half, theirs, 0, keepdims=False), axis, 2
        )
        other = swapped(share, axis, 2)
        first = jnp.where(mine == 0, share, other)
        second = jnp.where(mine == 0, other, share)
        return jnp.stack([first, second]), share
    half = (keep + swapped(send, axis, 1)).reshape(count, quarter, keep.shape[1])
    bit = 2
    while bit < size:
        half = half + swapped(half, axis, bit)
        bit *= 2
    return half, lax.dynamic_index_in_dim(half, mine, 0, keepdims=False)


def gathered_rows(half, axis):
    count, quarter, columns = half.shape
    odd = (lax.axis_index(axis) & 1) != 0
    other = swapped(half, axis, 1)
    low = jnp.where(odd, other, half)
    high = jnp.where(odd, half, other)
    return jnp.stack([low, high], axis=1).reshape(count * 2 * quarter, columns)


def coefficient_kernel(quarter, parity_ref, weight_ref, basis_ref, projector_ref, keep_ref, send_ref, total_ref):
    step = pl.program_id(0)
    scaled = (basis_ref[...].astype(jnp.float32) * weight_ref[...]).astype(jnp.bfloat16)
    product = lax.dot_general(
        scaled, projector_ref[...], (((1,), (1,)), ((), ())), preferred_element_type=jnp.float32
    )

    @pl.when(step == 0)
    def _():
        total_ref[...] = product

    @pl.when(step > 0)
    def _():
        total_ref[...] += product

    @pl.when(step == pl.num_programs(0) - 1)
    def _():
        count = keep_ref.shape[0] // quarter
        odd = parity_ref[0]
        for t in range(count):
            kept = pl.multiple_of((2 * t + odd) * quarter, 8)
            sent = pl.multiple_of((2 * t + 1 - odd) * quarter, 8)
            keep_ref[t * quarter : (t + 1) * quarter, :] = total_ref[pl.ds(kept, quarter), :]
            send_ref[t * quarter : (t + 1) * quarter, :] = total_ref[pl.ds(sent, quarter), :]


def partial_coefficients(flat_projectors, basis_t, weight, parity, quarter):
    rows, points = flat_projectors.shape
    width = basis_t.shape[0]
    depth = min(points, 4096)
    half = jax.ShapeDtypeStruct((width // 2, rows), jnp.float32)
    grid_spec = pltpu.PrefetchScalarGridSpec(
        num_scalar_prefetch=1,
        grid=(points // depth,),
        in_specs=[
            pl.BlockSpec((1, depth), lambda k, p: (0, k)),
            pl.BlockSpec((width, depth), lambda k, p: (0, k)),
            pl.BlockSpec((rows, depth), lambda k, p: (0, k)),
        ],
        out_specs=[
            pl.BlockSpec((width // 2, rows), lambda k, p: (0, 0)),
            pl.BlockSpec((width // 2, rows), lambda k, p: (0, 0)),
        ],
        scratch_shapes=[pltpu.VMEM((width, rows), jnp.float32)],
    )
    return pl.pallas_call(
        functools.partial(coefficient_kernel, quarter),
        out_shape=(half, half),
        grid_spec=grid_spec,
        compiler_params=pltpu.CompilerParams(dimension_semantics=("arbitrary",)),
        cost_estimate=pl.CostEstimate(
            flops=2 * rows * points * width,
            bytes_accessed=2 * rows * points + 2 * points * width + 4 * points + 4 * rows * width,
            transcendentals=0,
        ),
    )(parity, weight.reshape(1, points), basis_t, flat_projectors)


def pair_block(left_t, right_t):
    return lax.dot_general(
        left_t, right_t, (((1,), (1,)), ((), ())), precision=lax.Precision.HIGH
    )


def local(basis, quad_weight, projectors, species, counts, gamma_table):
    width = basis.shape[2]
    groups, atoms, slots, points = projectors.shape[1:]
    span = atoms * slots
    quarter = width // lax.axis_size("cuts")
    parity = (lax.axis_index("cuts") % 2).astype(jnp.int32).reshape(1)
    keep, send = partial_coefficients(
        projectors[0].reshape(groups * span, points), basis[0].T, quad_weight[0], parity, quarter
    )
    onehot = (
        species[0][:, None] == jnp.arange(gamma_table.shape[0], dtype=jnp.int32)[None, :]
    ).astype(jnp.float32)
    table = jnp.dot(onehot, gamma_table, precision=lax.Precision.HIGHEST)
    active = (jnp.arange(slots, dtype=jnp.int32)[None, :] < counts[0][:, None]).astype(jnp.float32)
    energy = (table * active).reshape(span)

    half, share = summed_rows(keep, send, "cuts")
    energy_row = jnp.pad(energy, (0, span))[None]
    to_right = jnp.concatenate([share[:, span:], energy_row], axis=0)
    to_left = jnp.concatenate([share[:, : 2 * span], energy_row], axis=0)
    from_left = passed_along(to_right, "elem", 1)
    from_right = passed_along(to_left, "elem", -1)
    full_t = gathered_rows(half, "cuts")

    left_energy = from_left[quarter, :span]
    right_energy = from_right[quarter, :span]
    weight_left = jnp.concatenate([left_energy, energy])
    weight_diag = jnp.concatenate([left_energy, energy, right_energy])
    weight_right = jnp.concatenate([energy, right_energy])
    block_left = pair_block(full_t[:, : 2 * span], from_left[:quarter] * weight_left[None])
    block_diag = pair_block(full_t, share * weight_diag[None])
    block_right = pair_block(full_t[:, span:], from_right[:quarter] * weight_right[None])
    owners = lax.axis_size("elem")
    stacked = jnp.stack([block_left, block_diag, block_right], axis=0)
    pieces = stacked.reshape(3, owners, width // owners, quarter).transpose(1, 0, 2, 3)
    received = lax.all_to_all(pieces.reshape(owners, -1), "elem", split_axis=0, concat_axis=0, tiled=True)
    return received.reshape(pieces.shape)


def solution(mesh):
    in_specs = (
        P("elem", "cuts", None),
        P("elem", "cuts"),
        P("elem", None, None, None, "cuts"),
        P("elem", None),
        P("elem", None),
        P(),
    )
    out_specs = P(None, None, "elem", "cuts")
    return jax.shard_map(local, mesh=mesh, in_specs=in_specs, out_specs=out_specs, check_vma=False)
```

```python
import functools

import jax
import jax.numpy as jnp
from jax import lax
from jax.experimental import pallas as pl
from jax.experimental.pallas import tpu as pltpu
from jax.sharding import PartitionSpec as P


def passed_along(block, axis, distance):
    devices = range(lax.axis_size(axis))
    route = [((i - distance) % len(devices), i) for i in devices]
    return lax.ppermute(block, axis, route)


def swapped(block, axis, bit):
    devices = range(lax.axis_size(axis))
    return lax.ppermute(block, axis, [(i, i ^ bit) for i in devices])


def summed_rows(keep, send, axis):
    size = lax.axis_size(axis)
    me = lax.axis_index(axis)
    count = size // 2
    quarter = keep.shape[0] // count
    mine = me // 2
    if count == 2:
        theirs = 1 - mine
        half = (keep + swapped(send, axis, 1)).reshape(count, quarter, keep.shape[1])
        share = lax.dynamic_index_in_dim(half, mine, 0, keepdims=False) + swapped(
            lax.dynamic_index_in_dim(half, theirs, 0, keepdims=False), axis, 2
        )
        beside = swapped(share, axis, 1)
        odd = (me & 1) != 0
        here = jnp.stack([jnp.where(odd, beside, share), jnp.where(odd, share, beside)])
        there = swapped(here, axis, 2)
        whole = jnp.where(mine == 0, jnp.stack([here, there]), jnp.stack([there, here]))
        return whole.reshape(size * quarter, keep.shape[1]), share
    half = (keep + swapped(send, axis, 1)).reshape(count, quarter, keep.shape[1])
    bit = 2
    while bit < size:
        half = half + swapped(half, axis, bit)
        bit *= 2
    return half, lax.dynamic_index_in_dim(half, mine, 0, keepdims=False)


def gathered_rows(half, axis):
    count, quarter, columns = half.shape
    odd = (lax.axis_index(axis) & 1) != 0
    other = swapped(half, axis, 1)
    low = jnp.where(odd, other, half)
    high = jnp.where(odd, half, other)
    return jnp.stack([low, high], axis=1).reshape(count * 2 * quarter, columns)


def coefficient_kernel(quarter, parity_ref, weight_ref, basis_ref, projector_ref, keep_ref, send_ref, total_ref):
    step = pl.program_id(0)
    scaled = (basis_ref[...].astype(jnp.float32) * weight_ref[...]).astype(jnp.bfloat16)
    product = lax.dot_general(
        scaled, projector_ref[...], (((1,), (1,)), ((), ())), preferred_element_type=jnp.float32
    )

    @pl.when(step == 0)
    def _():
        total_ref[...] = product

    @pl.when(step > 0)
    def _():
        total_ref[...] += product

    @pl.when(step == pl.num_programs(0) - 1)
    def _():
        count = keep_ref.shape[0] // quarter
        odd = parity_ref[0]
        for t in range(count):
            kept = pl.multiple_of((2 * t + odd) * quarter, 8)
            sent = pl.multiple_of((2 * t + 1 - odd) * quarter, 8)
            keep_ref[t * quarter : (t + 1) * quarter, :] = total_ref[pl.ds(kept, quarter), :]
            send_ref[t * quarter : (t + 1) * quarter, :] = total_ref[pl.ds(sent, quarter), :]


def partial_coefficients(flat_projectors, basis_t, weight, parity, quarter):
    rows, points = flat_projectors.shape
    width = basis_t.shape[0]
    depth = min(points, 4096)
    half = jax.ShapeDtypeStruct((width // 2, rows), jnp.float32)
    grid_spec = pltpu.PrefetchScalarGridSpec(
        num_scalar_prefetch=1,
        grid=(points // depth,),
        in_specs=[
            pl.BlockSpec((1, depth), lambda k, p: (0, k)),
            pl.BlockSpec((width, depth), lambda k, p: (0, k)),
            pl.BlockSpec((rows, depth), lambda k, p: (0, k)),
        ],
        out_specs=[
            pl.BlockSpec((width // 2, rows), lambda k, p: (0, 0)),
            pl.BlockSpec((width // 2, rows), lambda k, p: (0, 0)),
        ],
        scratch_shapes=[pltpu.VMEM((width, rows), jnp.float32)],
    )
    return pl.pallas_call(
        functools.partial(coefficient_kernel, quarter),
        out_shape=(half, half),
        grid_spec=grid_spec,
        compiler_params=pltpu.CompilerParams(dimension_semantics=("arbitrary",)),
        cost_estimate=pl.CostEstimate(
            flops=2 * rows * points * width,
            bytes_accessed=2 * rows * points + 2 * points * width + 4 * points + 4 * rows * width,
            transcendentals=0,
        ),
    )(parity, weight.reshape(1, points), basis_t, flat_projectors)


def pair_block(left_t, right_t):
    return lax.dot_general(
        left_t, right_t, (((1,), (1,)), ((), ())), precision=lax.Precision.HIGH
    )


def local(basis, quad_weight, projectors, species, counts, gamma_table):
    width = basis.shape[2]
    groups, atoms, slots, points = projectors.shape[1:]
    span = atoms * slots
    quarter = width // lax.axis_size("cuts")
    parity = (lax.axis_index("cuts") % 2).astype(jnp.int32).reshape(1)
    keep, send = partial_coefficients(
        projectors[0].reshape(groups * span, points), basis[0].T, quad_weight[0], parity, quarter
    )
    onehot = (
        species[0][:, None] == jnp.arange(gamma_table.shape[0], dtype=jnp.int32)[None, :]
    ).astype(jnp.float32)
    table = jnp.dot(onehot, gamma_table, precision=lax.Precision.HIGHEST)
    active = (jnp.arange(slots, dtype=jnp.int32)[None, :] < counts[0][:, None]).astype(jnp.float32)
    energy = (table * active).reshape(span)

    half, share = summed_rows(keep, send, "cuts")
    energy_row = jnp.pad(energy, (0, span))[None]
    to_right = jnp.concatenate([share[:, span:], energy_row], axis=0)
    to_left = jnp.concatenate([share[:, : 2 * span], energy_row], axis=0)
    from_left = passed_along(to_right, "elem", 1)
    from_right = passed_along(to_left, "elem", -1)
    full_t = half if half.ndim == 2 else gathered_rows(half, "cuts")

    left_energy = from_left[quarter, :span]
    right_energy = from_right[quarter, :span]
    weight_left = jnp.concatenate([left_energy, energy])
    weight_diag = jnp.concatenate([left_energy, energy, right_energy])
    weight_right = jnp.concatenate([energy, right_energy])
    block_left = pair_block(full_t[:, : 2 * span], from_left[:quarter] * weight_left[None])
    block_diag = pair_block(full_t, share * weight_diag[None])
    block_right = pair_block(full_t[:, span:], from_right[:quarter] * weight_right[None])
    owners = lax.axis_size("elem")
    stacked = jnp.stack([block_left, block_diag, block_right], axis=0)
    pieces = stacked.reshape(3, owners, width // owners, quarter).transpose(1, 0, 2, 3)
    received = lax.all_to_all(pieces.reshape(owners, -1), "elem", split_axis=0, concat_axis=0, tiled=True)
    return received.reshape(pieces.shape)


def solution(mesh):
    in_specs = (
        P("elem", "cuts", None),
        P("elem", "cuts"),
        P("elem", None, None, None, "cuts"),
        P("elem", None),
        P("elem", None),
        P(),
    )
    out_specs = P(None, None, "elem", "cuts")
    return jax.shard_map(local, mesh=mesh, in_specs=in_specs, out_specs=out_specs, check_vma=False)
```

```python
import functools

import jax
import jax.numpy as jnp
from jax import lax
from jax.experimental import pallas as pl
from jax.experimental.pallas import tpu as pltpu
from jax.sharding import PartitionSpec as P


def passed_along(block, axis, distance):
    devices = range(lax.axis_size(axis))
    route = [((i - distance) % len(devices), i) for i in devices]
    return lax.ppermute(block, axis, route)


def swapped(block, axis, bit):
    devices = range(lax.axis_size(axis))
    return lax.ppermute(block, axis, [(i, i ^ bit) for i in devices])


def summed_rows(keep, send, axis):
    size = lax.axis_size(axis)
    me = lax.axis_index(axis)
    count = size // 2
    quarter = keep.shape[0] // count
    mine = me // 2
    if count == 2:
        theirs = 1 - mine
        half = (keep + swapped(send, axis, 1)).reshape(count, quarter, keep.shape[1])
        share = lax.dynamic_index_in_dim(half, mine, 0, keepdims=False) + swapped(
            lax.dynamic_index_in_dim(half, theirs, 0, keepdims=False), axis, 2
        )
        other = swapped(share, axis, 2)
        first = jnp.where(mine == 0, share, other)
        second = jnp.where(mine == 0, other, share)
        return jnp.stack([first, second]), share
    half = (keep + swapped(send, axis, 1)).reshape(count, quarter, keep.shape[1])
    bit = 2
    while bit < size:
        half = half + swapped(half, axis, bit)
        bit *= 2
    return half, lax.dynamic_index_in_dim(half, mine, 0, keepdims=False)


def gathered_rows(half, axis):
    count, quarter, columns = half.shape
    odd = (lax.axis_index(axis) & 1) != 0
    other = swapped(half, axis, 1)
    low = jnp.where(odd, other, half)
    high = jnp.where(odd, half, other)
    return jnp.stack([low, high], axis=1).reshape(count * 2 * quarter, columns)


def coefficient_kernel(quarter, parity_ref, weight_ref, basis_ref, projector_ref, keep_ref, send_ref):
    step = pl.program_id(0)
    scaled = (basis_ref[...].astype(jnp.float32) * weight_ref[...]).astype(jnp.bfloat16)
    product = lax.dot_general(
        scaled, projector_ref[...], (((1,), (1,)), ((), ())), preferred_element_type=jnp.float32
    )
    odd = parity_ref[0] == 1
    count = keep_ref.shape[0] // quarter
    for t in range(count):
        even_rows = product[2 * t * quarter : (2 * t + 1) * quarter]
        odd_rows = product[(2 * t + 1) * quarter : (2 * t + 2) * quarter]
        rows = slice(t * quarter, (t + 1) * quarter)
        kept = jnp.where(odd, odd_rows, even_rows)
        sent = jnp.where(odd, even_rows, odd_rows)

        @pl.when(step == 0)
        def _():
            keep_ref[rows, :] = kept
            send_ref[rows, :] = sent

        @pl.when(step > 0)
        def _():
            keep_ref[rows, :] += kept
            send_ref[rows, :] += sent


def partial_coefficients(flat_projectors, basis_t, weight, parity, quarter):
    rows, points = flat_projectors.shape
    width = basis_t.shape[0]
    depth = min(points, 4096)
    half = jax.ShapeDtypeStruct((width // 2, rows), jnp.float32)
    grid_spec = pltpu.PrefetchScalarGridSpec(
        num_scalar_prefetch=1,
        grid=(points // depth,),
        in_specs=[
            pl.BlockSpec((1, depth), lambda k, p: (0, k)),
            pl.BlockSpec((width, depth), lambda k, p: (0, k)),
            pl.BlockSpec((rows, depth), lambda k, p: (0, k)),
        ],
        out_specs=[
            pl.BlockSpec((width // 2, rows), lambda k, p: (0, 0)),
            pl.BlockSpec((width // 2, rows), lambda k, p: (0, 0)),
        ],
    )
    return pl.pallas_call(
        functools.partial(coefficient_kernel, quarter),
        out_shape=(half, half),
        grid_spec=grid_spec,
        compiler_params=pltpu.CompilerParams(dimension_semantics=("arbitrary",)),
        cost_estimate=pl.CostEstimate(
            flops=2 * rows * points * width,
            bytes_accessed=2 * rows * points + 2 * points * width + 4 * points + 4 * rows * width,
            transcendentals=0,
        ),
    )(parity, weight.reshape(1, points), basis_t, flat_projectors)


def pair_block(left_t, right_t):
    return lax.dot_general(
        left_t, right_t, (((1,), (1,)), ((), ())), precision=lax.Precision.HIGH
    )


def local(basis, quad_weight, projectors, species, counts, gamma_table):
    width = basis.shape[2]
    groups, atoms, slots, points = projectors.shape[1:]
    span = atoms * slots
    quarter = width // lax.axis_size("cuts")
    parity = (lax.axis_index("cuts") % 2).astype(jnp.int32).reshape(1)
    keep, send = partial_coefficients(
        projectors[0].reshape(groups * span, points), basis[0].T, quad_weight[0], parity, quarter
    )
    onehot = (
        species[0][:, None] == jnp.arange(gamma_table.shape[0], dtype=jnp.int32)[None, :]
    ).astype(jnp.float32)
    table = jnp.dot(onehot, gamma_table, precision=lax.Precision.HIGHEST)
    active = (jnp.arange(slots, dtype=jnp.int32)[None, :] < counts[0][:, None]).astype(jnp.float32)
    energy = (table * active).reshape(span)

    half, share = summed_rows(keep, send, "cuts")
    energy_row = jnp.pad(energy, (0, span))[None]
    to_right = jnp.concatenate([share[:, span:], energy_row], axis=0)
    to_left = jnp.concatenate([share[:, : 2 * span], energy_row], axis=0)
    from_left = passed_along(to_right, "elem", 1)
    from_right = passed_along(to_left, "elem", -1)
    full_t = gathered_rows(half, "cuts")

    left_energy = from_left[quarter, :span]
    right_energy = from_right[quarter, :span]
    weight_left = jnp.concatenate([left_energy, energy])
    weight_diag = jnp.concatenate([left_energy, energy, right_energy])
    weight_right = jnp.concatenate([energy, right_energy])
    block_left = pair_block(full_t[:, : 2 * span], from_left[:quarter] * weight_left[None])
    block_diag = pair_block(full_t, share * weight_diag[None])
    block_right = pair_block(full_t[:, span:], from_right[:quarter] * weight_right[None])
    owners = lax.axis_size("elem")
    stacked = jnp.stack([block_left, block_diag, block_right], axis=0)
    pieces = stacked.reshape(3, owners, width // owners, quarter).transpose(1, 0, 2, 3)
    received = lax.all_to_all(pieces.reshape(owners, -1), "elem", split_axis=0, concat_axis=0, tiled=True)
    return received.reshape(pieces.shape)


def solution(mesh):
    in_specs = (
        P("elem", "cuts", None),
        P("elem", "cuts"),
        P("elem", None, None, None, "cuts"),
        P("elem", None),
        P("elem", None),
        P(),
    )
    out_specs = P(None, None, "elem", "cuts")
    return jax.shard_map(local, mesh=mesh, in_specs=in_specs, out_specs=out_specs, check_vma=False)
```

```python
import functools

import jax
import jax.numpy as jnp
from jax import lax
from jax.experimental import pallas as pl
from jax.experimental.pallas import tpu as pltpu
from jax.sharding import PartitionSpec as P


def passed_along(block, axis, distance):
    devices = range(lax.axis_size(axis))
    route = [((i - distance) % len(devices), i) for i in devices]
    return lax.ppermute(block, axis, route)


def swapped(block, axis, bit):
    devices = range(lax.axis_size(axis))
    return lax.ppermute(block, axis, [(i, i ^ bit) for i in devices])


def summed_rows(keep, send, axis):
    size = lax.axis_size(axis)
    me = lax.axis_index(axis)
    count = size // 2
    quarter = keep.shape[0] // count
    mine = me // 2
    if count == 2:
        theirs = 1 - mine
        half = (keep + swapped(send, axis, 1)).reshape(count, quarter, keep.shape[1])
        share = lax.dynamic_index_in_dim(half, mine, 0, keepdims=False) + swapped(
            lax.dynamic_index_in_dim(half, theirs, 0, keepdims=False), axis, 2
        )
        other = swapped(share, axis, 2)
        first = jnp.where(mine == 0, share, other)
        second = jnp.where(mine == 0, other, share)
        return jnp.stack([first, second]), share
    half = (keep + swapped(send, axis, 1)).reshape(count, quarter, keep.shape[1])
    bit = 2
    while bit < size:
        half = half + swapped(half, axis, bit)
        bit *= 2
    return half, lax.dynamic_index_in_dim(half, mine, 0, keepdims=False)


def gathered_rows(half, axis):
    count, quarter, columns = half.shape
    odd = (lax.axis_index(axis) & 1) != 0
    other = swapped(half, axis, 1)
    low = jnp.where(odd, other, half)
    high = jnp.where(odd, half, other)
    return jnp.stack([low, high], axis=1).reshape(count * 2 * quarter, columns)


def coefficient_kernel(quarter, parity_ref, weight_ref, basis_ref, projector_ref, keep_ref, send_ref):
    step = pl.program_id(0)
    scaled = (basis_ref[...].astype(jnp.float32) * weight_ref[...]).astype(jnp.bfloat16)
    product = lax.dot_general(
        scaled, projector_ref[...], (((1,), (1,)), ((), ())), preferred_element_type=jnp.float32
    )
    odd = parity_ref[0] == 1
    count = keep_ref.shape[0] // quarter
    for t in range(count):
        even_rows = product[2 * t * quarter : (2 * t + 1) * quarter]
        odd_rows = product[(2 * t + 1) * quarter : (2 * t + 2) * quarter]
        rows = slice(t * quarter, (t + 1) * quarter)
        kept = jnp.where(odd, odd_rows, even_rows)
        sent = jnp.where(odd, even_rows, odd_rows)

        @pl.when(step == 0)
        def _():
            keep_ref[rows, :] = kept
            send_ref[rows, :] = sent

        @pl.when(step > 0)
        def _():
            keep_ref[rows, :] += kept
            send_ref[rows, :] += sent


def partial_coefficients(flat_projectors, basis_t, weight, parity, quarter):
    rows, points = flat_projectors.shape
    width = basis_t.shape[0]
    depth = min(points, 2048)
    half = jax.ShapeDtypeStruct((width // 2, rows), jnp.float32)
    grid_spec = pltpu.PrefetchScalarGridSpec(
        num_scalar_prefetch=1,
        grid=(points // depth,),
        in_specs=[
            pl.BlockSpec((1, depth), lambda k, p: (0, k)),
            pl.BlockSpec((width, depth), lambda k, p: (0, k)),
            pl.BlockSpec((rows, depth), lambda k, p: (0, k)),
        ],
        out_specs=[
            pl.BlockSpec((width // 2, rows), lambda k, p: (0, 0)),
            pl.BlockSpec((width // 2, rows), lambda k, p: (0, 0)),
        ],
    )
    return pl.pallas_call(
        functools.partial(coefficient_kernel, quarter),
        out_shape=(half, half),
        grid_spec=grid_spec,
        compiler_params=pltpu.CompilerParams(dimension_semantics=("arbitrary",)),
        cost_estimate=pl.CostEstimate(
            flops=2 * rows * points * width,
            bytes_accessed=2 * rows * points + 2 * points * width + 4 * points + 4 * rows * width,
            transcendentals=0,
        ),
    )(parity, weight.reshape(1, points), basis_t, flat_projectors)


def pair_block(left_t, right_t):
    return lax.dot_general(
        left_t, right_t, (((1,), (1,)), ((), ())), precision=lax.Precision.HIGH
    )


def local(basis, quad_weight, projectors, species, counts, gamma_table):
    width = basis.shape[2]
    groups, atoms, slots, points = projectors.shape[1:]
    span = atoms * slots
    quarter = width // lax.axis_size("cuts")
    parity = (lax.axis_index("cuts") % 2).astype(jnp.int32).reshape(1)
    keep, send = partial_coefficients(
        projectors[0].reshape(groups * span, points), basis[0].T, quad_weight[0], parity, quarter
    )
    onehot = (
        species[0][:, None] == jnp.arange(gamma_table.shape[0], dtype=jnp.int32)[None, :]
    ).astype(jnp.float32)
    table = jnp.dot(onehot, gamma_table, precision=lax.Precision.HIGHEST)
    active = (jnp.arange(slots, dtype=jnp.int32)[None, :] < counts[0][:, None]).astype(jnp.float32)
    energy = (table * active).reshape(span)

    half, share = summed_rows(keep, send, "cuts")
    energy_row = jnp.pad(energy, (0, span))[None]
    to_right = jnp.concatenate([share[:, span:], energy_row], axis=0)
    to_left = jnp.concatenate([share[:, : 2 * span], energy_row], axis=0)
    from_left = passed_along(to_right, "elem", 1)
    from_right = passed_along(to_left, "elem", -1)
    full_t = gathered_rows(half, "cuts")

    left_energy = from_left[quarter, :span]
    right_energy = from_right[quarter, :span]
    weight_left = jnp.concatenate([left_energy, energy])
    weight_diag = jnp.concatenate([left_energy, energy, right_energy])
    weight_right = jnp.concatenate([energy, right_energy])
    block_left = pair_block(full_t[:, : 2 * span], from_left[:quarter] * weight_left[None])
    block_diag = pair_block(full_t, share * weight_diag[None])
    block_right = pair_block(full_t[:, span:], from_right[:quarter] * weight_right[None])
    owners = lax.axis_size("elem")
    stacked = jnp.stack([block_left, block_diag, block_right], axis=0)
    pieces = stacked.reshape(3, owners, width // owners, quarter).transpose(1, 0, 2, 3)
    received = lax.all_to_all(pieces.reshape(owners, -1), "elem", split_axis=0, concat_axis=0, tiled=True)
    return received.reshape(pieces.shape)


def solution(mesh):
    in_specs = (
        P("elem", "cuts", None),
        P("elem", "cuts"),
        P("elem", None, None, None, "cuts"),
        P("elem", None),
        P("elem", None),
        P(),
    )
    out_specs = P(None, None, "elem", "cuts")
    return jax.shard_map(local, mesh=mesh, in_specs=in_specs, out_specs=out_specs, check_vma=False)
```
